256 devices in a mesh: facet: 8 (over z), chan: 32 (over y, x, core).
Axes of the slice: x: 4, y: 4, z: 8, core: 2. Of those that a mesh axis runs over, the one named last changes fastest.
Arguments:
- sky_image: float32 [256, 32, 4096], P('chan', 'facet'), may hold values from -100 to 100
- dual_field: float32 [256, 32, 4096], P(None, 'facet', 'chan'), may hold values from -100 to 100
- sketch_matrix: bfloat16 [32, 4096, 128], P('facet', 'chan'), may hold values from -0.046875 to 0.046875
- grid_tiles: float32 [256, 4, 128, 128], P('chan'), may hold values from -0.5 to 0.5
- freq_block: int32 [256, 4], P('chan'), may hold values from 0 to 31
- vis_block: int32 [256, 4], P('chan'), may hold values from 0 to 3
- vis_data: float32 [256, 2, 32, 4, 128], P('chan', None, 'facet'), may hold values from -6 to 6
Outputs:
- new_image: float32 [256, 32, 4096], P('chan', 'facet')
- new_dual: float32 [256, 32, 4096], P(None, 'facet', 'chan')
The draws below stay inside these ranges and needn't reach their ends.
All inputs are finite; a program needn't handle non-finite values.
Results may differ from the reference program's by a relative error of at most 0.0003.
Values sent between devices are 32-bit elements; how exact they have to be, the bound alone decides.
No kernel may reach another device: no remote copies, remote signals or barrier semaphores. Data moves between devices by JAX's collectives and lax.ppermute only.
A program may use at most 128 MiB of HBM per device.

```python
import math
import jax
import jax.numpy as jnp
from jax import lax

CH = 256
W = 4096
BLOCK = 128
FB = 32
R = 4
ROWS = 32
TILES = 4
VB = 4
RANK = 128
SIGN_ITERS = 12
ROOT_ITERS = 14
N_FACET = 8


def scaled_field(key):
    subkeys = jax.random.split(key, 4)
    chan_scale = jnp.exp(jax.random.uniform(subkeys[0], (CH, 1, 1), jnp.float32, math.log(0.3), math.log(3.0)))
    rise_factor = 3.0
    noise_base = jax.random.truncated_normal(subkeys[3], -4.0, 4.0, (CH, ROWS, W), jnp.float32)
    column = jnp.arange(W, dtype=jnp.float32) / W
    col_scale = jnp.exp(math.log(rise_factor) * (column - 0.5) + jax.random.uniform(subkeys[1], (W,), jnp.float32, -0.6, 0.6))
    row_scale = jnp.exp(jax.random.uniform(subkeys[2], (1, ROWS, 1), jnp.float32, -0.4, 0.4))
    return chan_scale * row_scale * col_scale * noise_base


def draw_sky_image(key, part):
    return scaled_field(jax.random.fold_in(key, 11))


def draw_dual_field(key, part):
    return scaled_field(jax.random.fold_in(key, 23))


def place_ends(drawn, rng, least, largest):
    spot = [jax.random.randint(jax.random.fold_in(rng, axis), (), 0, length) for axis, length in enumerate(drawn.shape)]
    longest = drawn.shape.index(max(drawn.shape))
    next_to = spot[:longest] + [(spot[longest] + 1) % drawn.shape[longest]] + spot[longest + 1:]
    return drawn.at[tuple(spot)].set(least).at[tuple(next_to)].set(largest)


def steps_of(rng, dims, cuts, smallest, top_value):
    factor_of, own = 1.0, jax.random.fold_in(rng, 6)
    for dim, shards_of in cuts:
        heights = jnp.exp(jax.random.uniform(jax.random.fold_in(own, dim), (shards_of,), jnp.float32, smallest / len(cuts), top_value / len(cuts)))
        factor_of = factor_of * jnp.repeat(heights, dims[dim] // shards_of).reshape([-1 if axis == dim else 1 for axis in range(len(dims))])
    return factor_of


def centred(stream_key, shape, width, reach, cuts=(), kind=jnp.bfloat16):
    entries = width * jax.random.normal(stream_key, shape, jnp.float32)
    if cuts:
        entries = entries * steps_of(stream_key, shape, cuts, -0.22, 0.18)
    return jnp.clip(entries, -reach, reach).astype(kind)


def setup_inputs(seed: int = 0) -> dict:
    streams_of = jax.random.split(jax.random.key(seed), 8)
    return {
        "sky_image": draw_sky_image(jax.random.fold_in(streams_of[7], 71), 0),
        "dual_field": draw_dual_field(jax.random.fold_in(streams_of[7], 71), 0),
        "sketch_matrix": centred(streams_of[2], (ROWS, W, RANK), (R * W) ** -0.5, 0.046875, ((0, 8), (1, 32))),
        "grid_tiles": centred(streams_of[3], (CH, TILES, BLOCK, BLOCK), BLOCK ** -0.5, 0.5, ((0, 32),), jnp.float32),
        "freq_block": place_ends(jax.random.randint(streams_of[4], (CH, TILES), 0, W // BLOCK), jax.random.fold_in(streams_of[4], 1), 0, (W // BLOCK) - 1).astype(jnp.int32),
        "vis_block": place_ends(jax.random.randint(streams_of[5], (CH, TILES), 0, VB), jax.random.fold_in(streams_of[5], 1), 0, VB - 1).astype(jnp.int32),
        "vis_data": centred(streams_of[6], (CH, 2, ROWS, VB, BLOCK), 1.0, 6.0, ((0, 32), (2, 8)), jnp.float32),
    }


step_primal = 0.4
smooth_weight = 0.25
step_dual = 0.5
shrink_ratio = 0.25

def matmul_hi(first_mat, second_mat):
    return jnp.dot(first_mat, second_mat, precision=lax.Precision.HIGHEST)

def shrink_matrix(gram_mat):
    order_n = gram_mat.shape[0]
    identity = jnp.eye(order_n, dtype=gram_mat.dtype)
    thresh_sq = shrink_ratio * jnp.trace(gram_mat) / order_n
    shifted = gram_mat - thresh_sq * identity
    signum = shifted / jnp.sqrt(jnp.sum(shifted * shifted))

    def sign_step(turn_no, current):
        return 1.5 * current - 0.5 * matmul_hi(matmul_hi(current, current), current)
    signum = lax.fori_loop(0, SIGN_ITERS, sign_step, signum)
    keeper = 0.5 * (identity + signum)
    floored = 0.5 * (gram_mat + thresh_sq * identity + matmul_hi(shifted, signum))
    scale_c = jnp.sqrt(jnp.sum(floored * floored))

    def root_step(turn_no, state_pair):
        root_iter, inv_iter = state_pair
        step_mat = 0.5 * (3.0 * identity - matmul_hi(inv_iter, root_iter))
        return (matmul_hi(root_iter, step_mat), matmul_hi(step_mat, inv_iter))
    root_iter, inv_iter = lax.fori_loop(0, ROOT_ITERS, root_step, (floored / scale_c, identity))
    inv_root = inv_iter / jnp.sqrt(scale_c)
    return matmul_hi(keeper, identity - jnp.sqrt(thresh_sq) * inv_root)

def basis_from(sketch):
    lower_fac = jnp.linalg.cholesky(matmul_hi(sketch.T, sketch))
    return jax.scipy.linalg.solve_triangular(lower_fac, sketch.T, lower=True).T

def channel_gradient(pieces):
    rows_img, tile_set, freq_row, vis_row, vis_rows = pieces
    full_spec = jnp.fft.fft2(rows_img, norm='ortho')
    grid_spec = jnp.swapaxes(full_spec.reshape(ROWS, BLOCK, FB), 1, 2)
    spectra = jnp.stack([jnp.real(grid_spec), jnp.imag(grid_spec)]).astype(jnp.float32)
    pick_onehot = jax.nn.one_hot(freq_row, FB, dtype=jnp.float32)
    place_onehot = jax.nn.one_hot(vis_row, VB, dtype=jnp.float32)
    hi = lax.Precision.HIGHEST
    chosen = jnp.einsum('tb,xrbk->xtrk', pick_onehot, spectra, precision=hi)
    products = jnp.einsum('xtrk,tkm->xtrm', chosen, tile_set, precision=hi)
    predicted = jnp.einsum('tv,xtrm->xrvm', place_onehot, products, precision=hi)
    residual = predicted - vis_rows
    spread = jnp.einsum('tv,xrvm->xtrm', place_onehot, residual, precision=hi)
    pulled = jnp.einsum('xtrm,tkm->xtrk', spread, tile_set, precision=hi)
    back_spec = jnp.einsum('tb,xtrk->xrbk', pick_onehot, pulled, precision=hi)
    combined = lax.complex(back_spec[0], back_spec[1])
    flat_rows = jnp.swapaxes(combined, 1, 2).reshape(ROWS, W)
    return jnp.real(jnp.fft.ifft2(flat_rows, norm='ortho')).astype(jnp.float32)

def facet_dual(stacked):
    facet_field, sketch_rows = stacked
    flat_rows = facet_field.reshape(CH, R * W)
    sketch = matmul_hi(flat_rows, sketch_rows.reshape(R * W, RANK).astype(jnp.float32))
    basis_mat = basis_from(sketch)
    coords = matmul_hi(basis_mat.T, flat_rows)
    shrink = shrink_matrix(matmul_hi(coords, coords.T))
    return (flat_rows - matmul_hi(matmul_hi(basis_mat, shrink), coords)).reshape(CH, R, W)

def reference(sky_image, dual_field, sketch_matrix, grid_tiles, freq_block, vis_block, vis_data):
    gradient = lax.map(channel_gradient, (sky_image, grid_tiles, freq_block, vis_block, vis_data))
    padded = jnp.pad(sky_image, ((0, 0), (1, 1), (0, 0)))
    smooth = 2.0 * sky_image - padded[:, :-2] - padded[:, 2:]
    new_image = sky_image - step_primal * (gradient + smooth_weight * smooth + dual_field)
    merged = dual_field + step_dual * (2.0 * new_image - sky_image)
    facets = jnp.swapaxes(merged.reshape(CH, N_FACET, R, W), 0, 1)
    sketches = sketch_matrix.reshape(N_FACET, R, W, RANK)
    facet_out = lax.map(facet_dual, (facets, sketches))
    new_dual = jnp.swapaxes(facet_out, 0, 1).reshape(CH, ROWS, W)
    return (new_image, new_dual)
```

```python
import math

import jax
import jax.numpy as jnp
from jax import lax
from jax.sharding import PartitionSpec as P

SIGN_ITERS = 12
ROOT_ITERS = 14


step_primal = 0.4
smooth_weight = 0.25
step_dual = 0.5
shrink_ratio = 0.25

HI = lax.Precision.HIGHEST


def padded_2(block, sides, width):
    for axis, dim in sides:
        count = lax.axis_size(axis)
        forward = [(i, i + 1) for i in range(count - 1)]
        backward = [(target, source) for source, target in forward]
        low = lax.ppermute(
            lax.slice_in_dim(block, block.shape[dim] - width, None, axis=dim), axis, forward
        )
        high = lax.ppermute(lax.slice_in_dim(block, 0, width, axis=dim), axis, backward)
        block = jnp.concatenate([low, block, high], axis=dim)
    return block


def matmul_hi(first_mat, second_mat):
    return jnp.dot(first_mat, second_mat, precision=HI)


def shrink_matrix(gram_mat):
    order_n = gram_mat.shape[0]
    identity = jnp.eye(order_n, dtype=gram_mat.dtype)
    thresh_sq = shrink_ratio * jnp.trace(gram_mat) / order_n
    shifted = gram_mat - thresh_sq * identity
    signum = shifted / jnp.sqrt(jnp.sum(shifted * shifted))

    def sign_step(turn_no, current):
        return 1.5 * current - 0.5 * matmul_hi(matmul_hi(current, current), current)

    signum = lax.fori_loop(0, SIGN_ITERS, sign_step, signum)
    keeper = 0.5 * (identity + signum)
    floored = 0.5 * (gram_mat + thresh_sq * identity + matmul_hi(shifted, signum))
    scale_c = jnp.sqrt(jnp.sum(floored * floored))

    def root_step(turn_no, state_pair):
        root_iter, inv_iter = state_pair
        step_mat = 0.5 * (3.0 * identity - matmul_hi(inv_iter, root_iter))
        return (matmul_hi(root_iter, step_mat), matmul_hi(step_mat, inv_iter))

    root_iter, inv_iter = lax.fori_loop(0, ROOT_ITERS, root_step, (floored / scale_c, identity))
    inv_root = inv_iter / jnp.sqrt(scale_c)
    return matmul_hi(keeper, identity - jnp.sqrt(thresh_sq) * inv_root)


def phase_of(index, period):
    angle = (2.0 * math.pi / period) * (index % period).astype(jnp.float32)
    return jnp.cos(angle), jnp.sin(angle)


def data_gradient(sky_image, grid_tiles, freq_block, vis_block, vis_all):
    chan_count, row_count, width = sky_image.shape
    block = grid_tiles.shape[2]
    blocks_n = width // block
    all_rows = vis_all.shape[2]
    vb_n = vis_all.shape[3]
    row0 = lax.axis_index("facet") * row_count

    p_idx = lax.broadcasted_iota(jnp.int32, (row_count, all_rows), 1)
    q_idx = lax.broadcasted_iota(jnp.int32, (row_count, all_rows), 0) + row0
    cos_c, sin_c = phase_of(p_idx * q_idx, all_rows)
    col_scale = 1.0 / math.sqrt(all_rows)
    v_re = vis_all[:, 0]
    v_im = vis_all[:, 1]
    u_re = (
        jnp.einsum("qp,cpvm->cvqm", cos_c, v_re, precision=HI)
        - jnp.einsum("qp,cpvm->cvqm", sin_c, v_im, precision=HI)
    ) * col_scale
    u_im = (
        jnp.einsum("qp,cpvm->cvqm", sin_c, v_re, precision=HI)
        + jnp.einsum("qp,cpvm->cvqm", cos_c, v_im, precision=HI)
    ) * col_scale

    n2_idx = lax.broadcasted_iota(jnp.int32, freq_block.shape + (blocks_n,), 2)
    w_cos, w_sin = phase_of(freq_block[:, :, None] * n2_idx, blocks_n)
    n1_idx = lax.broadcasted_iota(jnp.int32, freq_block.shape + (block,), 2)
    t_cos, t_sin = phase_of(freq_block[:, :, None] * n1_idx, width)
    t_cos = t_cos[:, :, None, :]
    t_sin = t_sin[:, :, None, :]
    j_idx = lax.broadcasted_iota(jnp.int32, (block, block), 0)
    m_idx = lax.broadcasted_iota(jnp.int32, (block, block), 1)
    f_cos, f_sin = phase_of(j_idx * m_idx, block)
    row_scale = 1.0 / math.sqrt(width)

    x = sky_image.reshape(chan_count, row_count, blocks_n, block)
    y_re = jnp.einsum("ctn,crnm->ctrm", w_cos, x, precision=HI)
    y_im = -jnp.einsum("ctn,crnm->ctrm", w_sin, x, precision=HI)
    yt_re = y_re * t_cos + y_im * t_sin
    yt_im = y_im * t_cos - y_re * t_sin
    tiles_n = freq_block.shape[1]
    flat = chan_count * tiles_n * row_count
    yt_re = yt_re.reshape(flat, block)
    yt_im = yt_im.reshape(flat, block)
    s_re = (matmul_hi(yt_re, f_cos) + matmul_hi(yt_im, f_sin)) * row_scale
    s_im = (matmul_hi(yt_im, f_cos) - matmul_hi(yt_re, f_sin)) * row_scale
    s_re = s_re.reshape(chan_count, tiles_n, row_count, block)
    s_im = s_im.reshape(chan_count, tiles_n, row_count, block)
    z_re = jnp.einsum("ctrj,ctjm->ctrm", s_re, grid_tiles, precision=HI)
    z_im = jnp.einsum("ctrj,ctjm->ctrm", s_im, grid_tiles, precision=HI)
    place = jax.nn.one_hot(vis_block, vb_n, dtype=jnp.float32)
    r_re = jnp.einsum("ctv,ctrm->cvrm", place, z_re, precision=HI) - u_re
    r_im = jnp.einsum("ctv,ctrm->cvrm", place, z_im, precision=HI) - u_im
    sp_re = jnp.einsum("ctv,cvrm->ctrm", place, r_re, precision=HI)
    sp_im = jnp.einsum("ctv,cvrm->ctrm", place, r_im, precision=HI)
    c_re = jnp.einsum("ctrm,ctjm->ctrj", sp_re, grid_tiles, precision=HI)
    c_im = jnp.einsum("ctrm,ctjm->ctrj", sp_im, grid_tiles, precision=HI)
    c_re = c_re.reshape(flat, block)
    c_im = c_im.reshape(flat, block)
    d_re = (matmul_hi(c_re, f_cos) - matmul_hi(c_im, f_sin)) * row_scale
    d_im = (matmul_hi(c_re, f_sin) + matmul_hi(c_im, f_cos)) * row_scale
    d_re = d_re.reshape(chan_count, tiles_n, row_count, block)
    d_im = d_im.reshape(chan_count, tiles_n, row_count, block)
    dt_re = d_re * t_cos - d_im * t_sin
    dt_im = d_im * t_cos + d_re * t_sin
    grad = jnp.einsum("ctn,ctrm->crnm", w_cos, dt_re, precision=HI) - jnp.einsum(
        "ctn,ctrm->crnm", w_sin, dt_im, precision=HI
    )
    return grad.reshape(chan_count, row_count, width)


def on_device(sky_image, dual_field, sketch_matrix, grid_tiles, freq_block, vis_block, vis_data):
    dual_chan = lax.all_to_all(dual_field, "chan", split_axis=0, concat_axis=2, tiled=True)
    vis_all = lax.all_gather(vis_data, "facet", axis=2, tiled=True)
    padded = padded_2(sky_image, (("facet", 1),), 1)
    gradient = data_gradient(sky_image, grid_tiles, freq_block, vis_block, vis_all)
    smooth = 2.0 * sky_image - padded[:, :-2] - padded[:, 2:]
    new_image = sky_image - step_primal * (gradient + smooth_weight * smooth + dual_chan)
    rest = (1.0 - step_dual) * sky_image - 2.0 * step_dual * step_primal * (
        gradient + smooth_weight * smooth
    )
    rest_pix = lax.all_to_all(rest, "chan", split_axis=2, concat_axis=0, tiled=True)
    pixels = (1.0 - 2.0 * step_dual * step_primal) * dual_field + rest_pix
    chans = pixels.shape[0]
    flat_pix = pixels.reshape(chans, -1)
    sketch_rows = sketch_matrix.astype(jnp.float32).reshape(flat_pix.shape[1], -1)
    rank = sketch_rows.shape[1]
    part = jnp.concatenate(
        [matmul_hi(flat_pix, sketch_rows), jnp.dot(flat_pix, flat_pix.T, precision=HI)], axis=1
    )
    total = lax.psum(part, "chan")
    sketch = total[:, :rank]
    outer = total[:, rank:]
    lower_fac = jnp.linalg.cholesky(matmul_hi(sketch.T, sketch))
    basis_mat = jax.scipy.linalg.solve_triangular(lower_fac, sketch.T, lower=True).T
    gram_mat = matmul_hi(basis_mat.T, matmul_hi(outer, basis_mat))
    shrink = shrink_matrix(gram_mat)
    coords = matmul_hi(basis_mat.T, flat_pix)
    new_dual = flat_pix - matmul_hi(matmul_hi(basis_mat, shrink), coords)
    return (new_image, new_dual.reshape(pixels.shape))


def solution(mesh):
    placed = (
        P("chan", "facet", None),
        P(None, "facet", "chan"),
        P("facet", "chan", None),
        P("chan", None, None, None),
        P("chan", None),
        P("chan", None),
        P("chan", None, "facet", None, None),
    )
    return jax.shard_map(
        on_device,
        mesh=mesh,
        in_specs=placed,
        out_specs=(P("chan", "facet", None), P(None, "facet", "chan")),
        check_vma=False,
    )
```

```python
import math

import jax
import jax.numpy as jnp
from jax import lax
from jax.sharding import PartitionSpec as P

SIGN_ITERS = 12
ROOT_ITERS = 14


step_primal = 0.4
smooth_weight = 0.25
step_dual = 0.5
shrink_ratio = 0.25

HI = lax.Precision.HIGHEST


def padded_2(block, sides, width):
    for axis, dim in sides:
        count = lax.axis_size(axis)
        forward = [(i, i + 1) for i in range(count - 1)]
        backward = [(target, source) for source, target in forward]
        low = lax.ppermute(
            lax.slice_in_dim(block, block.shape[dim] - width, None, axis=dim), axis, forward
        )
        high = lax.ppermute(lax.slice_in_dim(block, 0, width, axis=dim), axis, backward)
        block = jnp.concatenate([low, block, high], axis=dim)
    return block


def matmul_hi(first_mat, second_mat):
    return jnp.dot(first_mat, second_mat, precision=HI)


def shrink_matrix(gram_mat):
    order_n = gram_mat.shape[0]
    identity = jnp.eye(order_n, dtype=gram_mat.dtype)
    thresh_sq = shrink_ratio * jnp.trace(gram_mat) / order_n
    shifted = gram_mat - thresh_sq * identity
    signum = shifted / jnp.sqrt(jnp.sum(shifted * shifted))

    def sign_step(turn_no, current):
        return 1.5 * current - 0.5 * matmul_hi(matmul_hi(current, current), current)

    signum = lax.fori_loop(0, SIGN_ITERS, sign_step, signum)
    keeper = 0.5 * (identity + signum)
    floored = 0.5 * (gram_mat + thresh_sq * identity + matmul_hi(shifted, signum))
    scale_c = jnp.sqrt(jnp.sum(floored * floored))

    def root_step(turn_no, state_pair):
        root_iter, inv_iter = state_pair
        step_mat = 0.5 * (3.0 * identity - matmul_hi(inv_iter, root_iter))
        return (matmul_hi(root_iter, step_mat), matmul_hi(step_mat, inv_iter))

    root_iter, inv_iter = lax.fori_loop(0, ROOT_ITERS, root_step, (floored / scale_c, identity))
    inv_root = inv_iter / jnp.sqrt(scale_c)
    return matmul_hi(keeper, identity - jnp.sqrt(thresh_sq) * inv_root)


def phase_of(index, period):
    angle = (2.0 * math.pi / period) * (index % period).astype(jnp.float32)
    return jnp.cos(angle), jnp.sin(angle)


def butterfly_sum(value, axis):
    count = lax.axis_size(axis)
    dist = 1
    while dist < count:
        pairs = [(i, i ^ dist) for i in range(count)]
        value = value + lax.ppermute(value, axis, pairs)
        dist *= 2
    return value


def doubling_gather(value, axis):
    count = lax.axis_size(axis)
    me = lax.axis_index(axis)
    have = value[None]
    dist = 1
    while dist < count:
        pairs = [(i, i ^ dist) for i in range(count)]
        other = lax.ppermute(have, axis, pairs)
        low_side = (me & dist) == 0
        have = jnp.where(
            low_side,
            jnp.concatenate([have, other], 0),
            jnp.concatenate([other, have], 0),
        )
        dist *= 2
    return have


def data_gradient(sky_b, grid_tiles, freq_block, vis_block, vis_all):
    blocks_n, chan_count, row_count, block = sky_b.shape
    width = blocks_n * block
    n_facet = vis_all.shape[0]
    all_rows = n_facet * vis_all.shape[3]
    vb_n = vis_all.shape[4]
    row0 = lax.axis_index("facet") * row_count

    p_idx = lax.broadcasted_iota(jnp.int32, (row_count, n_facet, vis_all.shape[3]), 1) * vis_all.shape[
        3
    ] + lax.broadcasted_iota(jnp.int32, (row_count, n_facet, vis_all.shape[3]), 2)
    q_idx = lax.broadcasted_iota(jnp.int32, (row_count, n_facet, vis_all.shape[3]), 0) + row0
    cos_c, sin_c = phase_of(p_idx * q_idx, all_rows)
    col_scale = 1.0 / math.sqrt(all_rows)
    v_re = vis_all[:, :, 0]
    v_im = vis_all[:, :, 1]
    u_re = (
        jnp.einsum("qfp,fcpvm->cvqm", cos_c, v_re, precision=HI)
        - jnp.einsum("qfp,fcpvm->cvqm", sin_c, v_im, precision=HI)
    ) * col_scale
    u_im = (
        jnp.einsum("qfp,fcpvm->cvqm", sin_c, v_re, precision=HI)
        + jnp.einsum("qfp,fcpvm->cvqm", cos_c, v_im, precision=HI)
    ) * col_scale

    n2_idx = lax.broadcasted_iota(jnp.int32, freq_block.shape + (blocks_n,), 2)
    w_cos, w_sin = phase_of(freq_block[:, :, None] * n2_idx, blocks_n)
    n1_idx = lax.broadcasted_iota(jnp.int32, freq_block.shape + (block,), 2)
    t_cos, t_sin = phase_of(freq_block[:, :, None] * n1_idx, width)
    t_cos = t_cos[:, :, None, :]
    t_sin = t_sin[:, :, None, :]
    j_idx = lax.broadcasted_iota(jnp.int32, (block, block), 0)
    m_idx = lax.broadcasted_iota(jnp.int32, (block, block), 1)
    f_cos, f_sin = phase_of(j_idx * m_idx, block)
    row_scale = 1.0 / math.sqrt(width)

    y_re = jnp.einsum("ctn,ncrm->ctrm", w_cos, sky_b, precision=HI)
    y_im = -jnp.einsum("ctn,ncrm->ctrm", w_sin, sky_b, precision=HI)
    yt_re = y_re * t_cos + y_im * t_sin
    yt_im = y_im * t_cos - y_re * t_sin
    tiles_n = freq_block.shape[1]
    flat = chan_count * tiles_n * row_count
    yt_re = yt_re.reshape(flat, block)
    yt_im = yt_im.reshape(flat, block)
    s_re = (matmul_hi(yt_re, f_cos) + matmul_hi(yt_im, f_sin)) * row_scale
    s_im = (matmul_hi(yt_im, f_cos) - matmul_hi(yt_re, f_sin)) * row_scale
    s_re = s_re.reshape(chan_count, tiles_n, row_count, block)
    s_im = s_im.reshape(chan_count, tiles_n, row_count, block)
    z_re = jnp.einsum("ctrj,ctjm->ctrm", s_re, grid_tiles, precision=HI)
    z_im = jnp.einsum("ctrj,ctjm->ctrm", s_im, grid_tiles, precision=HI)
    place = jax.nn.one_hot(vis_block, vb_n, dtype=jnp.float32)
    r_re = jnp.einsum("ctv,ctrm->cvrm", place, z_re, precision=HI) - u_re
    r_im = jnp.einsum("ctv,ctrm->cvrm", place, z_im, precision=HI) - u_im
    sp_re = jnp.einsum("ctv,cvrm->ctrm", place, r_re, precision=HI)
    sp_im = jnp.einsum("ctv,cvrm->ctrm", place, r_im, precision=HI)
    c_re = jnp.einsum("ctrm,ctjm->ctrj", sp_re, grid_tiles, precision=HI)
    c_im = jnp.einsum("ctrm,ctjm->ctrj", sp_im, grid_tiles, precision=HI)
    c_re = c_re.reshape(flat, block)
    c_im = c_im.reshape(flat, block)
    d_re = (matmul_hi(c_re, f_cos) - matmul_hi(c_im, f_sin)) * row_scale
    d_im = (matmul_hi(c_re, f_sin) + matmul_hi(c_im, f_cos)) * row_scale
    d_re = d_re.reshape(chan_count, tiles_n, row_count, block)
    d_im = d_im.reshape(chan_count, tiles_n, row_count, block)
    dt_re = d_re * t_cos - d_im * t_sin
    dt_im = d_im * t_cos + d_re * t_sin
    return jnp.einsum("ctn,ctrm->ncrm", w_cos, dt_re, precision=HI) - jnp.einsum(
        "ctn,ctrm->ncrm", w_sin, dt_im, precision=HI
    )


def on_device(sky_image, dual_field, sketch_matrix, grid_tiles, freq_block, vis_block, vis_data):
    chan_count, row_count, width = sky_image.shape
    block = grid_tiles.shape[2]
    blocks_n = width // block
    dual_b = lax.all_to_all(
        dual_field.reshape(blocks_n, chan_count, row_count, block), "chan", 0, 0, tiled=True
    )
    vis_all = doubling_gather(vis_data, "facet")
    sky_b = jnp.transpose(sky_image.reshape(chan_count, row_count, blocks_n, block), (2, 0, 1, 3))
    padded = padded_2(sky_b, (("facet", 2),), 1)
    grad_b = data_gradient(sky_b, grid_tiles, freq_block, vis_block, vis_all)
    smooth = 2.0 * sky_b - padded[:, :, :-2] - padded[:, :, 2:]
    new_b = sky_b - step_primal * (grad_b + smooth_weight * smooth + dual_b)
    new_image = jnp.transpose(new_b, (1, 2, 0, 3)).reshape(chan_count, row_count, width)
    rest = (1.0 - step_dual) * sky_b - 2.0 * step_dual * step_primal * (
        grad_b + smooth_weight * smooth
    )
    rest_pix = lax.all_to_all(rest, "chan", 0, 0, tiled=True).reshape(dual_field.shape)
    pixels = (1.0 - 2.0 * step_dual * step_primal) * dual_field + rest_pix
    chans = pixels.shape[0]
    flat_pix = pixels.reshape(chans, -1)
    sketch_rows = sketch_matrix.astype(jnp.float32).reshape(flat_pix.shape[1], -1)
    rank = sketch_rows.shape[1]
    part = jnp.concatenate(
        [matmul_hi(flat_pix, sketch_rows), jnp.dot(flat_pix, flat_pix.T, precision=HI)], axis=1
    )
    total = butterfly_sum(part, "chan")
    sketch = total[:, :rank]
    outer = total[:, rank:]
    lower_fac = jnp.linalg.cholesky(matmul_hi(sketch.T, sketch))
    basis_mat = jax.scipy.linalg.solve_triangular(lower_fac, sketch.T, lower=True).T
    gram_mat = matmul_hi(basis_mat.T, matmul_hi(outer, basis_mat))
    shrink = shrink_matrix(gram_mat)
    coords = matmul_hi(basis_mat.T, flat_pix)
    new_dual = flat_pix - matmul_hi(matmul_hi(basis_mat, shrink), coords)
    return (new_image, new_dual.reshape(pixels.shape))


def solution(mesh):
    placed = (
        P("chan", "facet", None),
        P(None, "facet", "chan"),
        P("facet", "chan", None),
        P("chan", None, None, None),
        P("chan", None),
        P("chan", None),
        P("chan", None, "facet", None, None),
    )
    return jax.shard_map(
        on_device,
        mesh=mesh,
        in_specs=placed,
        out_specs=(P("chan", "facet", None), P(None, "facet", "chan")),
        check_vma=False,
    )
```

```python
import math

import jax
import jax.numpy as jnp
from jax import lax
from jax.sharding import PartitionSpec as P

SIGN_ITERS = 12
ROOT_ITERS = 14


step_primal = 0.4
smooth_weight = 0.25
step_dual = 0.5
shrink_ratio = 0.25

HI = lax.Precision.HIGHEST


def padded_2(block, sides, width):
    for axis, dim in sides:
        count = lax.axis_size(axis)
        forward = [(i, i + 1) for i in range(count - 1)]
        backward = [(target, source) for source, target in forward]
        low = lax.ppermute(
            lax.slice_in_dim(block, block.shape[dim] - width, None, axis=dim), axis, forward
        )
        high = lax.ppermute(lax.slice_in_dim(block, 0, width, axis=dim), axis, backward)
        block = jnp.concatenate([low, block, high], axis=dim)
    return block


def matmul_hi(first_mat, second_mat):
    return jnp.dot(first_mat, second_mat, precision=HI)


def shrink_matrix(gram_mat):
    order_n = gram_mat.shape[0]
    identity = jnp.eye(order_n, dtype=gram_mat.dtype)
    thresh_sq = shrink_ratio * jnp.trace(gram_mat) / order_n
    shifted = gram_mat - thresh_sq * identity
    signum = shifted / jnp.sqrt(jnp.sum(shifted * shifted))

    def sign_step(turn_no, current):
        return 1.5 * current - 0.5 * matmul_hi(matmul_hi(current, current), current)

    signum = lax.fori_loop(0, SIGN_ITERS, sign_step, signum)
    keeper = 0.5 * (identity + signum)
    floored = 0.5 * (gram_mat + thresh_sq * identity + matmul_hi(shifted, signum))
    scale_c = jnp.sqrt(jnp.sum(floored * floored))

    def root_step(turn_no, state_pair):
        root_iter, inv_iter = state_pair
        step_mat = 0.5 * (3.0 * identity - matmul_hi(inv_iter, root_iter))
        return (matmul_hi(root_iter, step_mat), matmul_hi(step_mat, inv_iter))

    root_iter, inv_iter = lax.fori_loop(0, ROOT_ITERS, root_step, (floored / scale_c, identity))
    inv_root = inv_iter / jnp.sqrt(scale_c)
    return matmul_hi(keeper, identity - jnp.sqrt(thresh_sq) * inv_root)


def phase_of(index, period):
    angle = (2.0 * math.pi / period) * (index % period).astype(jnp.float32)
    return jnp.cos(angle), jnp.sin(angle)


def halving_sum(value, axis):
    count = lax.axis_size(axis)
    me = lax.axis_index(axis)
    dists = []
    dist = 1
    while dist < count:
        dists.append(dist)
        dist *= 2
    for dist in dists:
        pairs = [(i, i ^ dist) for i in range(count)]
        high = (me & dist) != 0
        half = value.shape[0] // 2
        low_part, high_part = value[:half], value[half:]
        keep = jnp.where(high, high_part, low_part)
        send = jnp.where(high, low_part, high_part)
        value = keep + lax.ppermute(send, axis, pairs)
    for dist in reversed(dists):
        pairs = [(i, i ^ dist) for i in range(count)]
        high = (me & dist) != 0
        other = lax.ppermute(value, axis, pairs)
        value = jnp.where(
            high, jnp.concatenate([other, value], 0), jnp.concatenate([value, other], 0)
        )
    return value


def ring_gather(value, axis):
    count = lax.axis_size(axis)
    to_right = [(i, (i + 1) % count) for i in range(count)]
    to_left = [(i, (i - 1) % count) for i in range(count)]
    slots = [None] * count
    slots[0] = value
    from_left = value
    from_right = value
    for step in range(1, count // 2 + 1):
        from_left = lax.ppermute(from_left, axis, to_right)
        slots[(count - step) % count] = from_left
        if step < count - step:
            from_right = lax.ppermute(from_right, axis, to_left)
            slots[step] = from_right
    return jnp.stack(slots, 0)


def data_gradient(sky_b, grid_tiles, freq_block, vis_block, vis_all):
    blocks_n, chan_count, row_count, block = sky_b.shape
    width = blocks_n * block
    n_facet = vis_all.shape[0]
    all_rows = n_facet * vis_all.shape[3]
    vb_n = vis_all.shape[4]
    row0 = lax.axis_index("facet") * row_count

    me_facet = lax.axis_index("facet")
    slot_idx = lax.broadcasted_iota(jnp.int32, (row_count, n_facet, vis_all.shape[3]), 1)
    p_idx = ((slot_idx + me_facet) % n_facet) * vis_all.shape[3] + lax.broadcasted_iota(
        jnp.int32, (row_count, n_facet, vis_all.shape[3]), 2
    )
    q_idx = lax.broadcasted_iota(jnp.int32, (row_count, n_facet, vis_all.shape[3]), 0) + row0
    cos_c, sin_c = phase_of(p_idx * q_idx, all_rows)
    col_scale = 1.0 / math.sqrt(all_rows)
    v_re = vis_all[:, :, 0]
    v_im = vis_all[:, :, 1]
    u_re = (
        jnp.einsum("qfp,fcpvm->cvqm", cos_c, v_re, precision=HI)
        - jnp.einsum("qfp,fcpvm->cvqm", sin_c, v_im, precision=HI)
    ) * col_scale
    u_im = (
        jnp.einsum("qfp,fcpvm->cvqm", sin_c, v_re, precision=HI)
        + jnp.einsum("qfp,fcpvm->cvqm", cos_c, v_im, precision=HI)
    ) * col_scale

    n2_idx = lax.broadcasted_iota(jnp.int32, freq_block.shape + (blocks_n,), 2)
    w_cos, w_sin = phase_of(freq_block[:, :, None] * n2_idx, blocks_n)
    n1_idx = lax.broadcasted_iota(jnp.int32, freq_block.shape + (block,), 2)
    t_cos, t_sin = phase_of(freq_block[:, :, None] * n1_idx, width)
    t_cos = t_cos[:, :, None, :]
    t_sin = t_sin[:, :, None, :]
    j_idx = lax.broadcasted_iota(jnp.int32, (block, block), 0)
    m_idx = lax.broadcasted_iota(jnp.int32, (block, block), 1)
    f_cos, f_sin = phase_of(j_idx * m_idx, block)
    row_scale = 1.0 / math.sqrt(width)

    y_re = jnp.einsum("ctn,ncrm->ctrm", w_cos, sky_b, precision=HI)
    y_im = -jnp.einsum("ctn,ncrm->ctrm", w_sin, sky_b, precision=HI)
    yt_re = y_re * t_cos + y_im * t_sin
    yt_im = y_im * t_cos - y_re * t_sin
    tiles_n = freq_block.shape[1]
    flat = chan_count * tiles_n * row_count
    yt_re = yt_re.reshape(flat, block)
    yt_im = yt_im.reshape(flat, block)
    s_re = (matmul_hi(yt_re, f_cos) + matmul_hi(yt_im, f_sin)) * row_scale
    s_im = (matmul_hi(yt_im, f_cos) - matmul_hi(yt_re, f_sin)) * row_scale
    s_re = s_re.reshape(chan_count, tiles_n, row_count, block)
    s_im = s_im.reshape(chan_count, tiles_n, row_count, block)
    z_re = jnp.einsum("ctrj,ctjm->ctrm", s_re, grid_tiles, precision=HI)
    z_im = jnp.einsum("ctrj,ctjm->ctrm", s_im, grid_tiles, precision=HI)
    place = jax.nn.one_hot(vis_block, vb_n, dtype=jnp.float32)
    r_re = jnp.einsum("ctv,ctrm->cvrm", place, z_re, precision=HI) - u_re
    r_im = jnp.einsum("ctv,ctrm->cvrm", place, z_im, precision=HI) - u_im
    sp_re = jnp.einsum("ctv,cvrm->ctrm", place, r_re, precision=HI)
    sp_im = jnp.einsum("ctv,cvrm->ctrm", place, r_im, precision=HI)
    c_re = jnp.einsum("ctrm,ctjm->ctrj", sp_re, grid_tiles, precision=HI)
    c_im = jnp.einsum("ctrm,ctjm->ctrj", sp_im, grid_tiles, precision=HI)
    c_re = c_re.reshape(flat, block)
    c_im = c_im.reshape(flat, block)
    d_re = (matmul_hi(c_re, f_cos) - matmul_hi(c_im, f_sin)) * row_scale
    d_im = (matmul_hi(c_re, f_sin) + matmul_hi(c_im, f_cos)) * row_scale
    d_re = d_re.reshape(chan_count, tiles_n, row_count, block)
    d_im = d_im.reshape(chan_count, tiles_n, row_count, block)
    dt_re = d_re * t_cos - d_im * t_sin
    dt_im = d_im * t_cos + d_re * t_sin
    return jnp.einsum("ctn,ctrm->ncrm", w_cos, dt_re, precision=HI) - jnp.einsum(
        "ctn,ctrm->ncrm", w_sin, dt_im, precision=HI
    )


def on_device(sky_image, dual_field, sketch_matrix, grid_tiles, freq_block, vis_block, vis_data):
    chan_count, row_count, width = sky_image.shape
    block = grid_tiles.shape[2]
    blocks_n = width // block
    dual_b = lax.all_to_all(
        dual_field.reshape(blocks_n, chan_count, row_count, block), "chan", 0, 0, tiled=True
    )
    vis_all = ring_gather(vis_data, "facet")
    sky_b = jnp.transpose(sky_image.reshape(chan_count, row_count, blocks_n, block), (2, 0, 1, 3))
    padded = padded_2(sky_b, (("facet", 2),), 1)
    grad_b = data_gradient(sky_b, grid_tiles, freq_block, vis_block, vis_all)
    smooth = 2.0 * sky_b - padded[:, :, :-2] - padded[:, :, 2:]
    new_b = sky_b - step_primal * (grad_b + smooth_weight * smooth + dual_b)
    new_image = jnp.transpose(new_b, (1, 2, 0, 3)).reshape(chan_count, row_count, width)
    rest = (1.0 - step_dual) * sky_b - 2.0 * step_dual * step_primal * (
        grad_b + smooth_weight * smooth
    )
    rest_pix = lax.all_to_all(rest, "chan", 0, 0, tiled=True).reshape(dual_field.shape)
    pixels = (1.0 - 2.0 * step_dual * step_primal) * dual_field + rest_pix
    chans = pixels.shape[0]
    flat_pix = pixels.reshape(chans, -1)
    sketch_rows = sketch_matrix.astype(jnp.float32).reshape(flat_pix.shape[1], -1)
    rank = sketch_rows.shape[1]
    part = jnp.concatenate(
        [matmul_hi(flat_pix, sketch_rows), jnp.dot(flat_pix, flat_pix.T, precision=HI)], axis=1
    )
    total = halving_sum(part, "chan")
    sketch = total[:, :rank]
    outer = total[:, rank:]
    lower_fac = jnp.linalg.cholesky(matmul_hi(sketch.T, sketch))
    basis_mat = jax.scipy.linalg.solve_triangular(lower_fac, sketch.T, lower=True).T
    gram_mat = matmul_hi(basis_mat.T, matmul_hi(outer, basis_mat))
    shrink = shrink_matrix(gram_mat)
    coords = matmul_hi(basis_mat.T, flat_pix)
    new_dual = flat_pix - matmul_hi(matmul_hi(basis_mat, shrink), coords)
    return (new_image, new_dual.reshape(pixels.shape))


def solution(mesh):
    placed = (
        P("chan", "facet", None),
        P(None, "facet", "chan"),
        P("facet", "chan", None),
        P("chan", None, None, None),
        P("chan", None),
        P("chan", None),
        P("chan", None, "facet", None, None),
    )
    return jax.shard_map(
        on_device,
        mesh=mesh,
        in_specs=placed,
        out_specs=(P("chan", "facet", None), P(None, "facet", "chan")),
        check_vma=False,
    )
```

```python
import math

import jax
import jax.numpy as jnp
from jax import lax
from jax.sharding import PartitionSpec as P

SIGN_ITERS = 12
ROOT_ITERS = 14


step_primal = 0.4
smooth_weight = 0.25
step_dual = 0.5
shrink_ratio = 0.25

HI = lax.Precision.HIGHEST


def padded_2(block, sides, width):
    for axis, dim in sides:
        count = lax.axis_size(axis)
        forward = [(i, i + 1) for i in range(count - 1)]
        backward = [(target, source) for source, target in forward]
        low = lax.ppermute(
            lax.slice_in_dim(block, block.shape[dim] - width, None, axis=dim), axis, forward
        )
        high = lax.ppermute(lax.slice_in_dim(block, 0, width, axis=dim), axis, backward)
        block = jnp.concatenate([low, block, high], axis=dim)
    return block


def matmul_hi(first_mat, second_mat):
    return jnp.dot(first_mat, second_mat, precision=HI)


def shrink_matrix(gram_mat):
    order_n = gram_mat.shape[0]
    identity = jnp.eye(order_n, dtype=gram_mat.dtype)
    thresh_sq = shrink_ratio * jnp.trace(gram_mat) / order_n
    shifted = gram_mat - thresh_sq * identity
    signum = shifted / jnp.sqrt(jnp.sum(shifted * shifted))

    def sign_step(turn_no, current):
        return 1.5 * current - 0.5 * matmul_hi(matmul_hi(current, current), current)

    signum = lax.fori_loop(0, SIGN_ITERS, sign_step, signum)
    keeper = 0.5 * (identity + signum)
    floored = 0.5 * (gram_mat + thresh_sq * identity + matmul_hi(shifted, signum))
    scale_c = jnp.sqrt(jnp.sum(floored * floored))

    def root_step(turn_no, state_pair):
        root_iter, inv_iter = state_pair
        step_mat = 0.5 * (3.0 * identity - matmul_hi(inv_iter, root_iter))
        return (matmul_hi(root_iter, step_mat), matmul_hi(step_mat, inv_iter))

    root_iter, inv_iter = lax.fori_loop(0, ROOT_ITERS, root_step, (floored / scale_c, identity))
    inv_root = inv_iter / jnp.sqrt(scale_c)
    return matmul_hi(keeper, identity - jnp.sqrt(thresh_sq) * inv_root)


def phase_of(index, period):
    angle = (2.0 * math.pi / period) * (index % period).astype(jnp.float32)
    return jnp.cos(angle), jnp.sin(angle)


def exchange_sum(value, axis):
    count = lax.axis_size(axis)
    rows = value.shape[0]
    pieces = value.reshape((count, rows // count) + value.shape[1:])
    mine = jnp.sum(lax.all_to_all(pieces, axis, 0, 0, tiled=True), axis=0)
    spread = jnp.broadcast_to(mine[None], pieces.shape)
    return lax.all_to_all(spread, axis, 0, 0, tiled=True).reshape(value.shape)


def exchange_gather(value, axis):
    count = lax.axis_size(axis)
    spread = jnp.broadcast_to(value[None], (count,) + value.shape)
    return lax.all_to_all(spread, axis, 0, 0, tiled=True)


def data_gradient(sky_b, grid_tiles, freq_block, vis_block, vis_all):
    blocks_n, chan_count, row_count, block = sky_b.shape
    width = blocks_n * block
    n_facet = vis_all.shape[0]
    all_rows = n_facet * vis_all.shape[3]
    vb_n = vis_all.shape[4]
    row0 = lax.axis_index("facet") * row_count

    p_idx = lax.broadcasted_iota(jnp.int32, (row_count, n_facet, vis_all.shape[3]), 1) * vis_all.shape[
        3
    ] + lax.broadcasted_iota(jnp.int32, (row_count, n_facet, vis_all.shape[3]), 2)
    q_idx = lax.broadcasted_iota(jnp.int32, (row_count, n_facet, vis_all.shape[3]), 0) + row0
    cos_c, sin_c = phase_of(p_idx * q_idx, all_rows)
    col_scale = 1.0 / math.sqrt(all_rows)
    v_re = vis_all[:, :, 0]
    v_im = vis_all[:, :, 1]
    u_re = (
        jnp.einsum("qfp,fcpvm->cvqm", cos_c, v_re, precision=HI)
        - jnp.einsum("qfp,fcpvm->cvqm", sin_c, v_im, precision=HI)
    ) * col_scale
    u_im = (
        jnp.einsum("qfp,fcpvm->cvqm", sin_c, v_re, precision=HI)
        + jnp.einsum("qfp,fcpvm->cvqm", cos_c, v_im, precision=HI)
    ) * col_scale

    n2_idx = lax.broadcasted_iota(jnp.int32, freq_block.shape + (blocks_n,), 2)
    w_cos, w_sin = phase_of(freq_block[:, :, None] * n2_idx, blocks_n)
    n1_idx = lax.broadcasted_iota(jnp.int32, freq_block.shape + (block,), 2)
    t_cos, t_sin = phase_of(freq_block[:, :, None] * n1_idx, width)
    t_cos = t_cos[:, :, None, :]
    t_sin = t_sin[:, :, None, :]
    j_idx = lax.broadcasted_iota(jnp.int32, (block, block), 0)
    m_idx = lax.broadcasted_iota(jnp.int32, (block, block), 1)
    f_cos, f_sin = phase_of(j_idx * m_idx, block)
    row_scale = 1.0 / math.sqrt(width)

    y_re = jnp.einsum("ctn,ncrm->ctrm", w_cos, sky_b, precision=HI)
    y_im = -jnp.einsum("ctn,ncrm->ctrm", w_sin, sky_b, precision=HI)
    yt_re = y_re * t_cos + y_im * t_sin
    yt_im = y_im * t_cos - y_re * t_sin
    tiles_n = freq_block.shape[1]
    flat = chan_count * tiles_n * row_count
    yt_re = yt_re.reshape(flat, block)
    yt_im = yt_im.reshape(flat, block)
    s_re = (matmul_hi(yt_re, f_cos) + matmul_hi(yt_im, f_sin)) * row_scale
    s_im = (matmul_hi(yt_im, f_cos) - matmul_hi(yt_re, f_sin)) * row_scale
    s_re = s_re.reshape(chan_count, tiles_n, row_count, block)
    s_im = s_im.reshape(chan_count, tiles_n, row_count, block)
    z_re = jnp.einsum("ctrj,ctjm->ctrm", s_re, grid_tiles, precision=HI)
    z_im = jnp.einsum("ctrj,ctjm->ctrm", s_im, grid_tiles, precision=HI)
    place = jax.nn.one_hot(vis_block, vb_n, dtype=jnp.float32)
    r_re = jnp.einsum("ctv,ctrm->cvrm", place, z_re, precision=HI) - u_re
    r_im = jnp.einsum("ctv,ctrm->cvrm", place, z_im, precision=HI) - u_im
    sp_re = jnp.einsum("ctv,cvrm->ctrm", place, r_re, precision=HI)
    sp_im = jnp.einsum("ctv,cvrm->ctrm", place, r_im, precision=HI)
    c_re = jnp.einsum("ctrm,ctjm->ctrj", sp_re, grid_tiles, precision=HI)
    c_im = jnp.einsum("ctrm,ctjm->ctrj", sp_im, grid_tiles, precision=HI)
    c_re = c_re.reshape(flat, block)
    c_im = c_im.reshape(flat, block)
    d_re = (matmul_hi(c_re, f_cos) - matmul_hi(c_im, f_sin)) * row_scale
    d_im = (matmul_hi(c_re, f_sin) + matmul_hi(c_im, f_cos)) * row_scale
    d_re = d_re.reshape(chan_count, tiles_n, row_count, block)
    d_im = d_im.reshape(chan_count, tiles_n, row_count, block)
    dt_re = d_re * t_cos - d_im * t_sin
    dt_im = d_im * t_cos + d_re * t_sin
    return jnp.einsum("ctn,ctrm->ncrm", w_cos, dt_re, precision=HI) - jnp.einsum(
        "ctn,ctrm->ncrm", w_sin, dt_im, precision=HI
    )


def on_device(sky_image, dual_field, sketch_matrix, grid_tiles, freq_block, vis_block, vis_data):
    chan_count, row_count, width = sky_image.shape
    block = grid_tiles.shape[2]
    blocks_n = width // block
    dual_b = lax.all_to_all(
        dual_field.reshape(blocks_n, chan_count, row_count, block), "chan", 0, 0, tiled=True
    )
    vis_all = exchange_gather(vis_data, "facet")
    sky_b = jnp.transpose(sky_image.reshape(chan_count, row_count, blocks_n, block), (2, 0, 1, 3))
    padded = padded_2(sky_b, (("facet", 2),), 1)
    grad_b = data_gradient(sky_b, grid_tiles, freq_block, vis_block, vis_all)
    smooth = 2.0 * sky_b - padded[:, :, :-2] - padded[:, :, 2:]
    new_b = sky_b - step_primal * (grad_b + smooth_weight * smooth + dual_b)
    new_image = jnp.transpose(new_b, (1, 2, 0, 3)).reshape(chan_count, row_count, width)
    rest = (1.0 - step_dual) * sky_b - 2.0 * step_dual * step_primal * (
        grad_b + smooth_weight * smooth
    )
    rest_pix = lax.all_to_all(rest, "chan", 0, 0, tiled=True).reshape(dual_field.shape)
    pixels = (1.0 - 2.0 * step_dual * step_primal) * dual_field + rest_pix
    chans = pixels.shape[0]
    flat_pix = pixels.reshape(chans, -1)
    sketch_rows = sketch_matrix.astype(jnp.float32).reshape(flat_pix.shape[1], -1)
    rank = sketch_rows.shape[1]
    part = jnp.concatenate(
        [matmul_hi(flat_pix, sketch_rows), jnp.dot(flat_pix, flat_pix.T, precision=HI)], axis=1
    )
    total = exchange_sum(part, "chan")
    sketch = total[:, :rank]
    outer = total[:, rank:]
    lower_fac = jnp.linalg.cholesky(matmul_hi(sketch.T, sketch))
    basis_mat = jax.scipy.linalg.solve_triangular(lower_fac, sketch.T, lower=True).T
    gram_mat = matmul_hi(basis_mat.T, matmul_hi(outer, basis_mat))
    shrink = shrink_matrix(gram_mat)
    coords = matmul_hi(basis_mat.T, flat_pix)
    new_dual = flat_pix - matmul_hi(matmul_hi(basis_mat, shrink), coords)
    return (new_image, new_dual.reshape(pixels.shape))


def solution(mesh):
    placed = (
        P("chan", "facet", None),
        P(None, "facet", "chan"),
        P("facet", "chan", None),
        P("chan", None, None, None),
        P("chan", None),
        P("chan", None),
        P("chan", None, "facet", None, None),
    )
    return jax.shard_map(
        on_device,
        mesh=mesh,
        in_specs=placed,
        out_specs=(P("chan", "facet", None), P(None, "facet", "chan")),
        check_vma=False,
    )
```

```python
import math

import jax
import jax.numpy as jnp
from jax import lax
from jax.sharding import PartitionSpec as P
from jax.experimental import pallas as pl
from jax.experimental.pallas import tpu as pltpu

SIGN_ITERS = 12
ROOT_ITERS = 14


step_primal = 0.4
smooth_weight = 0.25
step_dual = 0.5
shrink_ratio = 0.25

HI = lax.Precision.HIGHEST


def padded_2(block, sides, width):
    for axis, dim in sides:
        count = lax.axis_size(axis)
        forward = [(i, i + 1) for i in range(count - 1)]
        backward = [(target, source) for source, target in forward]
        low = lax.ppermute(
            lax.slice_in_dim(block, block.shape[dim] - width, None, axis=dim), axis, forward
        )
        high = lax.ppermute(lax.slice_in_dim(block, 0, width, axis=dim), axis, backward)
        block = jnp.concatenate([low, block, high], axis=dim)
    return block


def matmul_hi(first_mat, second_mat):
    return jnp.dot(first_mat, second_mat, precision=HI)


def shrink_matrix(gram_mat):
    order_n = gram_mat.shape[0]
    identity = jnp.eye(order_n, dtype=gram_mat.dtype)
    thresh_sq = shrink_ratio * jnp.trace(gram_mat) / order_n
    shifted = gram_mat - thresh_sq * identity
    signum = shifted / jnp.sqrt(jnp.sum(shifted * shifted))

    def sign_step(turn_no, current):
        return 1.5 * current - 0.5 * matmul_hi(matmul_hi(current, current), current)

    signum = lax.fori_loop(0, SIGN_ITERS, sign_step, signum)
    keeper = 0.5 * (identity + signum)
    floored = 0.5 * (gram_mat + thresh_sq * identity + matmul_hi(shifted, signum))
    scale_c = jnp.sqrt(jnp.sum(floored * floored))

    def root_step(turn_no, state_pair):
        root_iter, inv_iter = state_pair
        step_mat = 0.5 * (3.0 * identity - matmul_hi(inv_iter, root_iter))
        return (matmul_hi(root_iter, step_mat), matmul_hi(step_mat, inv_iter))

    root_iter, inv_iter = lax.fori_loop(0, ROOT_ITERS, root_step, (floored / scale_c, identity))
    inv_root = inv_iter / jnp.sqrt(scale_c)
    return matmul_hi(keeper, identity - jnp.sqrt(thresh_sq) * inv_root)


def _total(value):
    return jnp.sum(jnp.sum(value, axis=1, keepdims=True), axis=0, keepdims=True)


def _shrink_kernel(gram_ref, eye_ref, out_ref):
    gram_mat = gram_ref[...]
    order_n = gram_mat.shape[0]
    identity = eye_ref[...]

    def mm(first_mat, second_mat):
        return jnp.dot(first_mat, second_mat, precision=HI, preferred_element_type=jnp.float32)

    thresh_sq = shrink_ratio * _total(gram_mat * identity) / order_n
    shifted = gram_mat - thresh_sq * identity
    signum = shifted / jnp.sqrt(_total(shifted * shifted))

    def sign_step(turn_no, current):
        return 1.5 * current - 0.5 * mm(mm(current, current), current)

    for turn_no in range(SIGN_ITERS):
        signum = sign_step(turn_no, signum)
    keeper = 0.5 * (identity + signum)
    floored = 0.5 * (gram_mat + thresh_sq * identity + mm(shifted, signum))
    scale_c = jnp.sqrt(_total(floored * floored))

    def root_step(turn_no, state_pair):
        root_iter, inv_iter = state_pair
        step_mat = 0.5 * (3.0 * identity - mm(inv_iter, root_iter))
        return (mm(root_iter, step_mat), mm(step_mat, inv_iter))

    state_pair = (floored / scale_c, identity)
    for turn_no in range(ROOT_ITERS):
        state_pair = root_step(turn_no, state_pair)
    root_iter, inv_iter = state_pair
    inv_root = inv_iter / jnp.sqrt(scale_c)
    out_ref[...] = mm(keeper, identity - jnp.sqrt(thresh_sq) * inv_root)


def shrink_fused(gram_mat):
    order_n = gram_mat.shape[0]
    flops = 2 * order_n**3 * (2 * SIGN_ITERS + 3 * ROOT_ITERS + 2)
    return pl.pallas_call(
        _shrink_kernel,
        out_shape=jax.ShapeDtypeStruct(gram_mat.shape, jnp.float32),
        in_specs=[pl.BlockSpec(memory_space=pltpu.VMEM)] * 2,
        out_specs=pl.BlockSpec(memory_space=pltpu.VMEM),
        cost_estimate=pl.CostEstimate(flops=flops, transcendentals=4, bytes_accessed=12 * order_n * order_n),
    )(gram_mat, jnp.eye(order_n, dtype=jnp.float32))


def phase_of(index, period):
    angle = (2.0 * math.pi / period) * (index % period).astype(jnp.float32)
    return jnp.cos(angle), jnp.sin(angle)


def exchange_sum(value, axis):
    count = lax.axis_size(axis)
    rows = value.shape[0]
    pieces = value.reshape((count, rows // count) + value.shape[1:])
    mine = jnp.sum(lax.all_to_all(pieces, axis, 0, 0, tiled=True), axis=0)
    spread = jnp.broadcast_to(mine[None], pieces.shape)
    return lax.all_to_all(spread, axis, 0, 0, tiled=True).reshape(value.shape)


def exchange_gather(value, axis):
    count = lax.axis_size(axis)
    spread = jnp.broadcast_to(value[None], (count,) + value.shape)
    return lax.all_to_all(spread, axis, 0, 0, tiled=True)


def data_gradient(sky_b, grid_tiles, freq_block, vis_block, vis_all):
    blocks_n, chan_count, row_count, block = sky_b.shape
    width = blocks_n * block
    n_facet = vis_all.shape[0]
    all_rows = n_facet * vis_all.shape[3]
    vb_n = vis_all.shape[4]
    row0 = lax.axis_index("facet") * row_count

    p_idx = lax.broadcasted_iota(jnp.int32, (row_count, n_facet, vis_all.shape[3]), 1) * vis_all.shape[
        3
    ] + lax.broadcasted_iota(jnp.int32, (row_count, n_facet, vis_all.shape[3]), 2)
    q_idx = lax.broadcasted_iota(jnp.int32, (row_count, n_facet, vis_all.shape[3]), 0) + row0
    cos_c, sin_c = phase_of(p_idx * q_idx, all_rows)
    col_scale = 1.0 / math.sqrt(all_rows)
    v_re = vis_all[:, :, 0]
    v_im = vis_all[:, :, 1]
    u_re = (
        jnp.einsum("qfp,fcpvm->cvqm", cos_c, v_re, precision=HI)
        - jnp.einsum("qfp,fcpvm->cvqm", sin_c, v_im, precision=HI)
    ) * col_scale
    u_im = (
        jnp.einsum("qfp,fcpvm->cvqm", sin_c, v_re, precision=HI)
        + jnp.einsum("qfp,fcpvm->cvqm", cos_c, v_im, precision=HI)
    ) * col_scale

    n2_idx = lax.broadcasted_iota(jnp.int32, freq_block.shape + (blocks_n,), 2)
    w_cos, w_sin = phase_of(freq_block[:, :, None] * n2_idx, blocks_n)
    n1_idx = lax.broadcasted_iota(jnp.int32, freq_block.shape + (block,), 2)
    t_cos, t_sin = phase_of(freq_block[:, :, None] * n1_idx, width)
    t_cos = t_cos[:, :, None, :]
    t_sin = t_sin[:, :, None, :]
    j_idx = lax.broadcasted_iota(jnp.int32, (block, block), 0)
    m_idx = lax.broadcasted_iota(jnp.int32, (block, block), 1)
    f_cos, f_sin = phase_of(j_idx * m_idx, block)
    row_scale = 1.0 / math.sqrt(width)

    y_re = jnp.einsum("ctn,ncrm->ctrm", w_cos, sky_b, precision=HI)
    y_im = -jnp.einsum("ctn,ncrm->ctrm", w_sin, sky_b, precision=HI)
    yt_re = y_re * t_cos + y_im * t_sin
    yt_im = y_im * t_cos - y_re * t_sin
    tiles_n = freq_block.shape[1]
    flat = chan_count * tiles_n * row_count
    yt_re = yt_re.reshape(flat, block)
    yt_im = yt_im.reshape(flat, block)
    s_re = (matmul_hi(yt_re, f_cos) + matmul_hi(yt_im, f_sin)) * row_scale
    s_im = (matmul_hi(yt_im, f_cos) - matmul_hi(yt_re, f_sin)) * row_scale
    s_re = s_re.reshape(chan_count, tiles_n, row_count, block)
    s_im = s_im.reshape(chan_count, tiles_n, row_count, block)
    z_re = jnp.einsum("ctrj,ctjm->ctrm", s_re, grid_tiles, precision=HI)
    z_im = jnp.einsum("ctrj,ctjm->ctrm", s_im, grid_tiles, precision=HI)
    place = jax.nn.one_hot(vis_block, vb_n, dtype=jnp.float32)
    r_re = jnp.einsum("ctv,ctrm->cvrm", place, z_re, precision=HI) - u_re
    r_im = jnp.einsum("ctv,ctrm->cvrm", place, z_im, precision=HI) - u_im
    sp_re = jnp.einsum("ctv,cvrm->ctrm", place, r_re, precision=HI)
    sp_im = jnp.einsum("ctv,cvrm->ctrm", place, r_im, precision=HI)
    c_re = jnp.einsum("ctrm,ctjm->ctrj", sp_re, grid_tiles, precision=HI)
    c_im = jnp.einsum("ctrm,ctjm->ctrj", sp_im, grid_tiles, precision=HI)
    c_re = c_re.reshape(flat, block)
    c_im = c_im.reshape(flat, block)
    d_re = (matmul_hi(c_re, f_cos) - matmul_hi(c_im, f_sin)) * row_scale
    d_im = (matmul_hi(c_re, f_sin) + matmul_hi(c_im, f_cos)) * row_scale
    d_re = d_re.reshape(chan_count, tiles_n, row_count, block)
    d_im = d_im.reshape(chan_count, tiles_n, row_count, block)
    dt_re = d_re * t_cos - d_im * t_sin
    dt_im = d_im * t_cos + d_re * t_sin
    return jnp.einsum("ctn,ctrm->ncrm", w_cos, dt_re, precision=HI) - jnp.einsum(
        "ctn,ctrm->ncrm", w_sin, dt_im, precision=HI
    )


def on_device(sky_image, dual_field, sketch_matrix, grid_tiles, freq_block, vis_block, vis_data):
    chan_count, row_count, width = sky_image.shape
    block = grid_tiles.shape[2]
    blocks_n = width // block
    dual_b = lax.all_to_all(
        dual_field.reshape(blocks_n, chan_count, row_count, block), "chan", 0, 0, tiled=True
    )
    vis_all = exchange_gather(vis_data, "facet")
    sky_b = jnp.transpose(sky_image.reshape(chan_count, row_count, blocks_n, block), (2, 0, 1, 3))
    padded = padded_2(sky_b, (("facet", 2),), 1)
    grad_b = data_gradient(sky_b, grid_tiles, freq_block, vis_block, vis_all)
    smooth = 2.0 * sky_b - padded[:, :, :-2] - padded[:, :, 2:]
    new_b = sky_b - step_primal * (grad_b + smooth_weight * smooth + dual_b)
    new_image = jnp.transpose(new_b, (1, 2, 0, 3)).reshape(chan_count, row_count, width)
    rest = (1.0 - step_dual) * sky_b - 2.0 * step_dual * step_primal * (
        grad_b + smooth_weight * smooth
    )
    rest_pix = lax.all_to_all(rest, "chan", 0, 0, tiled=True).reshape(dual_field.shape)
    pixels = (1.0 - 2.0 * step_dual * step_primal) * dual_field + rest_pix
    chans = pixels.shape[0]
    flat_pix = pixels.reshape(chans, -1)
    sketch_rows = sketch_matrix.astype(jnp.float32).reshape(flat_pix.shape[1], -1)
    rank = sketch_rows.shape[1]
    part = jnp.concatenate(
        [matmul_hi(flat_pix, sketch_rows), jnp.dot(flat_pix, flat_pix.T, precision=HI)], axis=1
    )
    total = exchange_sum(part, "chan")
    sketch = total[:, :rank]
    outer = total[:, rank:]
    lower_fac = jnp.linalg.cholesky(matmul_hi(sketch.T, sketch))
    basis_mat = jax.scipy.linalg.solve_triangular(lower_fac, sketch.T, lower=True).T
    gram_mat = matmul_hi(basis_mat.T, matmul_hi(outer, basis_mat))
    shrink = shrink_fused(gram_mat)
    coords = matmul_hi(basis_mat.T, flat_pix)
    new_dual = flat_pix - matmul_hi(matmul_hi(basis_mat, shrink), coords)
    return (new_image, new_dual.reshape(pixels.shape))


def solution(mesh):
    placed = (
        P("chan", "facet", None),
        P(None, "facet", "chan"),
        P("facet", "chan", None),
        P("chan", None, None, None),
        P("chan", None),
        P("chan", None),
        P("chan", None, "facet", None, None),
    )
    return jax.shard_map(
        on_device,
        mesh=mesh,
        in_specs=placed,
        out_specs=(P("chan", "facet", None), P(None, "facet", "chan")),
        check_vma=False,
    )
```

```python
import math

import jax
import jax.numpy as jnp
from jax import lax
from jax.sharding import PartitionSpec as P


SIGN_ITERS = 12
ROOT_ITERS = 14


step_primal = 0.4
smooth_weight = 0.25
step_dual = 0.5
shrink_ratio = 0.25

HI = lax.Precision.HIGHEST


def padded_2(block, sides, width):
    for axis, dim in sides:
        count = lax.axis_size(axis)
        forward = [(i, i + 1) for i in range(count - 1)]
        backward = [(target, source) for source, target in forward]
        low = lax.ppermute(
            lax.slice_in_dim(block, block.shape[dim] - width, None, axis=dim), axis, forward
        )
        high = lax.ppermute(lax.slice_in_dim(block, 0, width, axis=dim), axis, backward)
        block = jnp.concatenate([low, block, high], axis=dim)
    return block


def matmul_hi(first_mat, second_mat):
    return jnp.dot(first_mat, second_mat, precision=HI)


def shrink_matrix(gram_mat):
    order_n = gram_mat.shape[0]
    identity = jnp.eye(order_n, dtype=gram_mat.dtype)
    thresh_sq = shrink_ratio * jnp.trace(gram_mat) / order_n
    shifted = gram_mat - thresh_sq * identity
    signum = shifted / jnp.sqrt(jnp.sum(shifted * shifted))

    def sign_step(turn_no, current):
        return 1.5 * current - 0.5 * matmul_hi(matmul_hi(current, current), current)

    signum = lax.fori_loop(0, SIGN_ITERS, sign_step, signum)
    keeper = 0.5 * (identity + signum)
    floored = 0.5 * (gram_mat + thresh_sq * identity + matmul_hi(shifted, signum))
    scale_c = jnp.sqrt(jnp.sum(floored * floored))

    def root_step(turn_no, state_pair):
        root_iter, inv_iter = state_pair
        step_mat = 0.5 * (3.0 * identity - matmul_hi(inv_iter, root_iter))
        return (matmul_hi(root_iter, step_mat), matmul_hi(step_mat, inv_iter))

    _, inv_iter = lax.fori_loop(0, ROOT_ITERS, root_step, (floored / scale_c, identity))
    inv_root = inv_iter / jnp.sqrt(scale_c)
    return matmul_hi(keeper, identity - jnp.sqrt(thresh_sq) * inv_root)


def phase_of(index, period):
    angle = (2.0 * math.pi / period) * (index % period).astype(jnp.float32)
    return jnp.cos(angle), jnp.sin(angle)


def exchange_sum(value, axis):
    count = lax.axis_size(axis)
    rows = value.shape[0]
    pieces = value.reshape((count, rows // count) + value.shape[1:])
    mine = jnp.sum(lax.all_to_all(pieces, axis, 0, 0, tiled=True), axis=0)
    spread = jnp.broadcast_to(mine[None], pieces.shape)
    return lax.all_to_all(spread, axis, 0, 0, tiled=True).reshape(value.shape)


def exchange_gather(value, axis):
    count = lax.axis_size(axis)
    spread = jnp.broadcast_to(value[None], (count,) + value.shape)
    return lax.all_to_all(spread, axis, 0, 0, tiled=True)


def data_gradient(sky_b, grid_tiles, freq_block, vis_block, vis_all):
    blocks_n, chan_count, row_count, block = sky_b.shape
    width = blocks_n * block
    n_facet = vis_all.shape[0]
    all_rows = n_facet * vis_all.shape[3]
    vb_n = vis_all.shape[4]
    row0 = lax.axis_index("facet") * row_count

    p_idx = lax.broadcasted_iota(jnp.int32, (row_count, n_facet, vis_all.shape[3]), 1) * vis_all.shape[
        3
    ] + lax.broadcasted_iota(jnp.int32, (row_count, n_facet, vis_all.shape[3]), 2)
    q_idx = lax.broadcasted_iota(jnp.int32, (row_count, n_facet, vis_all.shape[3]), 0) + row0
    cos_c, sin_c = phase_of(p_idx * q_idx, all_rows)
    col_scale = 1.0 / math.sqrt(all_rows)
    v_re = vis_all[:, :, 0]
    v_im = vis_all[:, :, 1]
    u_re = (
        jnp.einsum("qfp,fcpvm->cvqm", cos_c, v_re, precision=HI)
        - jnp.einsum("qfp,fcpvm->cvqm", sin_c, v_im, precision=HI)
    ) * col_scale
    u_im = (
        jnp.einsum("qfp,fcpvm->cvqm", sin_c, v_re, precision=HI)
        + jnp.einsum("qfp,fcpvm->cvqm", cos_c, v_im, precision=HI)
    ) * col_scale

    n2_idx = lax.broadcasted_iota(jnp.int32, freq_block.shape + (blocks_n,), 2)
    w_cos, w_sin = phase_of(freq_block[:, :, None] * n2_idx, blocks_n)
    n1_idx = lax.broadcasted_iota(jnp.int32, freq_block.shape + (block,), 2)
    t_cos, t_sin = phase_of(freq_block[:, :, None] * n1_idx, width)
    t_cos = t_cos[:, :, None, :]
    t_sin = t_sin[:, :, None, :]
    j_idx = lax.broadcasted_iota(jnp.int32, (block, block), 0)
    m_idx = lax.broadcasted_iota(jnp.int32, (block, block), 1)
    f_cos, f_sin = phase_of(j_idx * m_idx, block)
    row_scale = 1.0 / math.sqrt(width)

    y_re = jnp.einsum("ctn,ncrm->ctrm", w_cos, sky_b, precision=HI)
    y_im = -jnp.einsum("ctn,ncrm->ctrm", w_sin, sky_b, precision=HI)
    yt_re = y_re * t_cos + y_im * t_sin
    yt_im = y_im * t_cos - y_re * t_sin
    tiles_n = freq_block.shape[1]
    flat = chan_count * tiles_n * row_count
    yt_re = yt_re.reshape(flat, block)
    yt_im = yt_im.reshape(flat, block)
    s_re = (matmul_hi(yt_re, f_cos) + matmul_hi(yt_im, f_sin)) * row_scale
    s_im = (matmul_hi(yt_im, f_cos) - matmul_hi(yt_re, f_sin)) * row_scale
    s_re = s_re.reshape(chan_count, tiles_n, row_count, block)
    s_im = s_im.reshape(chan_count, tiles_n, row_count, block)
    z_re = jnp.einsum("ctrj,ctjm->ctrm", s_re, grid_tiles, precision=HI)
    z_im = jnp.einsum("ctrj,ctjm->ctrm", s_im, grid_tiles, precision=HI)
    place = jax.nn.one_hot(vis_block, vb_n, dtype=jnp.float32)
    r_re = jnp.einsum("ctv,ctrm->cvrm", place, z_re, precision=HI) - u_re
    r_im = jnp.einsum("ctv,ctrm->cvrm", place, z_im, precision=HI) - u_im
    sp_re = jnp.einsum("ctv,cvrm->ctrm", place, r_re, precision=HI)
    sp_im = jnp.einsum("ctv,cvrm->ctrm", place, r_im, precision=HI)
    c_re = jnp.einsum("ctrm,ctjm->ctrj", sp_re, grid_tiles, precision=HI)
    c_im = jnp.einsum("ctrm,ctjm->ctrj", sp_im, grid_tiles, precision=HI)
    c_re = c_re.reshape(flat, block)
    c_im = c_im.reshape(flat, block)
    d_re = (matmul_hi(c_re, f_cos) - matmul_hi(c_im, f_sin)) * row_scale
    d_im = (matmul_hi(c_re, f_sin) + matmul_hi(c_im, f_cos)) * row_scale
    d_re = d_re.reshape(chan_count, tiles_n, row_count, block)
    d_im = d_im.reshape(chan_count, tiles_n, row_count, block)
    dt_re = d_re * t_cos - d_im * t_sin
    dt_im = d_im * t_cos + d_re * t_sin
    return jnp.einsum("ctn,ctrm->ncrm", w_cos, dt_re, precision=HI) - jnp.einsum(
        "ctn,ctrm->ncrm", w_sin, dt_im, precision=HI
    )


def _on_device(sky_image, dual_field, sketch_matrix, grid_tiles, freq_block, vis_block, vis_data):
    chan_count, row_count, width = sky_image.shape
    block = grid_tiles.shape[2]
    blocks_n = width // block
    dual_b = lax.all_to_all(
        dual_field.reshape(blocks_n, chan_count, row_count, block), "chan", 0, 0, tiled=True
    )
    vis_all = exchange_gather(vis_data, "facet")
    sky_b = jnp.transpose(sky_image.reshape(chan_count, row_count, blocks_n, block), (2, 0, 1, 3))
    padded = padded_2(sky_b, (("facet", 2),), 1)
    grad_b = data_gradient(sky_b, grid_tiles, freq_block, vis_block, vis_all)
    smooth = 2.0 * sky_b - padded[:, :, :-2] - padded[:, :, 2:]
    new_b = sky_b - step_primal * (grad_b + smooth_weight * smooth + dual_b)
    new_image = jnp.transpose(new_b, (1, 2, 0, 3)).reshape(chan_count, row_count, width)
    rest = (1.0 - step_dual) * sky_b - 2.0 * step_dual * step_primal * (
        grad_b + smooth_weight * smooth
    )
    rest_pix = lax.all_to_all(rest, "chan", 0, 0, tiled=True).reshape(dual_field.shape)
    pixels = (1.0 - 2.0 * step_dual * step_primal) * dual_field + rest_pix
    chans = pixels.shape[0]
    flat_pix = pixels.reshape(chans, -1)
    sketch_rows = sketch_matrix.astype(jnp.float32).reshape(flat_pix.shape[1], -1)
    rank = sketch_rows.shape[1]
    part = jnp.concatenate(
        [matmul_hi(flat_pix, sketch_rows), jnp.dot(flat_pix, flat_pix.T, precision=HI)], axis=1
    )
    total = exchange_sum(part, "chan")
    sketch = total[:, :rank]
    outer = total[:, rank:]
    lower_fac = jnp.linalg.cholesky(matmul_hi(sketch.T, sketch))
    basis_mat = jax.scipy.linalg.solve_triangular(lower_fac, sketch.T, lower=True).T
    gram_mat = matmul_hi(basis_mat.T, matmul_hi(outer, basis_mat))
    shrink = shrink_matrix(gram_mat)
    coords = matmul_hi(basis_mat.T, flat_pix)
    new_dual = flat_pix - matmul_hi(matmul_hi(basis_mat, shrink), coords)
    return (new_image, new_dual.reshape(pixels.shape))


def solution(mesh):
    placed = (
        P("chan", "facet", None),
        P(None, "facet", "chan"),
        P("facet", "chan", None),
        P("chan", None, None, None),
        P("chan", None),
        P("chan", None),
        P("chan", None, "facet", None, None),
    )
    return jax.shard_map(
        _on_device,
        mesh=mesh,
        in_specs=placed,
        out_specs=(P("chan", "facet", None), P(None, "facet", "chan")),
        check_vma=False,
    )
```

```python
import math

import jax
import jax.numpy as jnp
from jax import lax
from jax.sharding import PartitionSpec as P


SIGN_ITERS = 12
ROOT_ITERS = 14


step_primal = 0.4
smooth_weight = 0.25
step_dual = 0.5
shrink_ratio = 0.25

HI = lax.Precision.HIGHEST


def padded_2(block, sides, width):
    for axis, dim in sides:
        count = lax.axis_size(axis)
        forward = [(i, i + 1) for i in range(count - 1)]
        backward = [(target, source) for source, target in forward]
        low = lax.ppermute(
            lax.slice_in_dim(block, block.shape[dim] - width, None, axis=dim), axis, forward
        )
        high = lax.ppermute(lax.slice_in_dim(block, 0, width, axis=dim), axis, backward)
        block = jnp.concatenate([low, block, high], axis=dim)
    return block


def matmul_hi(first_mat, second_mat):
    return jnp.dot(first_mat, second_mat, precision=HI)


def shrink_matrix(gram_mat):
    order_n = gram_mat.shape[0]
    identity = jnp.eye(order_n, dtype=gram_mat.dtype)
    thresh_sq = shrink_ratio * jnp.trace(gram_mat) / order_n
    shifted = gram_mat - thresh_sq * identity
    signum = shifted / jnp.sqrt(jnp.sum(shifted * shifted))

    def sign_step(turn_no, current):
        return 1.5 * current - 0.5 * matmul_hi(matmul_hi(current, current), current)

    signum = lax.fori_loop(0, SIGN_ITERS, sign_step, signum)
    keeper = 0.5 * (identity + signum)
    floored = 0.5 * (gram_mat + thresh_sq * identity + matmul_hi(shifted, signum))
    scale_c = jnp.sqrt(jnp.sum(floored * floored))

    def root_step(turn_no, stacked):
        root_iter, inv_iter = stacked[:order_n], stacked[order_n:]
        step_mat = 0.5 * (3.0 * identity - matmul_hi(inv_iter, root_iter))
        return matmul_hi(stacked, step_mat)

    stacked = lax.fori_loop(
        0, ROOT_ITERS, root_step, jnp.concatenate([floored / scale_c, identity], axis=0)
    )
    inv_iter = stacked[order_n:]
    inv_root = inv_iter / jnp.sqrt(scale_c)
    return matmul_hi(keeper, identity - jnp.sqrt(thresh_sq) * inv_root)


def phase_of(index, period):
    angle = (2.0 * math.pi / period) * (index % period).astype(jnp.float32)
    return jnp.cos(angle), jnp.sin(angle)


def exchange_sum(value, axis):
    count = lax.axis_size(axis)
    rows = value.shape[0]
    pieces = value.reshape((count, rows // count) + value.shape[1:])
    mine = jnp.sum(lax.all_to_all(pieces, axis, 0, 0, tiled=True), axis=0)
    spread = jnp.broadcast_to(mine[None], pieces.shape)
    return lax.all_to_all(spread, axis, 0, 0, tiled=True).reshape(value.shape)


def exchange_gather(value, axis):
    count = lax.axis_size(axis)
    spread = jnp.broadcast_to(value[None], (count,) + value.shape)
    return lax.all_to_all(spread, axis, 0, 0, tiled=True)


def data_gradient(sky_b, grid_tiles, freq_block, vis_block, vis_all):
    blocks_n, chan_count, row_count, block = sky_b.shape
    width = blocks_n * block
    n_facet = vis_all.shape[0]
    all_rows = n_facet * vis_all.shape[3]
    vb_n = vis_all.shape[4]
    row0 = lax.axis_index("facet") * row_count

    p_idx = lax.broadcasted_iota(jnp.int32, (row_count, n_facet, vis_all.shape[3]), 1) * vis_all.shape[
        3
    ] + lax.broadcasted_iota(jnp.int32, (row_count, n_facet, vis_all.shape[3]), 2)
    q_idx = lax.broadcasted_iota(jnp.int32, (row_count, n_facet, vis_all.shape[3]), 0) + row0
    cos_c, sin_c = phase_of(p_idx * q_idx, all_rows)
    col_scale = 1.0 / math.sqrt(all_rows)
    v_re = vis_all[:, :, 0]
    v_im = vis_all[:, :, 1]
    u_re = (
        jnp.einsum("qfp,fcpvm->cvqm", cos_c, v_re, precision=HI)
        - jnp.einsum("qfp,fcpvm->cvqm", sin_c, v_im, precision=HI)
    ) * col_scale
    u_im = (
        jnp.einsum("qfp,fcpvm->cvqm", sin_c, v_re, precision=HI)
        + jnp.einsum("qfp,fcpvm->cvqm", cos_c, v_im, precision=HI)
    ) * col_scale

    n2_idx = lax.broadcasted_iota(jnp.int32, freq_block.shape + (blocks_n,), 2)
    w_cos, w_sin = phase_of(freq_block[:, :, None] * n2_idx, blocks_n)
    n1_idx = lax.broadcasted_iota(jnp.int32, freq_block.shape + (block,), 2)
    t_cos, t_sin = phase_of(freq_block[:, :, None] * n1_idx, width)
    t_cos = t_cos[:, :, None, :]
    t_sin = t_sin[:, :, None, :]
    j_idx = lax.broadcasted_iota(jnp.int32, (block, block), 0)
    m_idx = lax.broadcasted_iota(jnp.int32, (block, block), 1)
    f_cos, f_sin = phase_of(j_idx * m_idx, block)
    row_scale = 1.0 / math.sqrt(width)

    y_re = jnp.einsum("ctn,ncrm->ctrm", w_cos, sky_b, precision=HI)
    y_im = -jnp.einsum("ctn,ncrm->ctrm", w_sin, sky_b, precision=HI)
    yt_re = y_re * t_cos + y_im * t_sin
    yt_im = y_im * t_cos - y_re * t_sin
    tiles_n = freq_block.shape[1]
    flat = chan_count * tiles_n * row_count
    yt_re = yt_re.reshape(flat, block)
    yt_im = yt_im.reshape(flat, block)
    s_re = (matmul_hi(yt_re, f_cos) + matmul_hi(yt_im, f_sin)) * row_scale
    s_im = (matmul_hi(yt_im, f_cos) - matmul_hi(yt_re, f_sin)) * row_scale
    s_re = s_re.reshape(chan_count, tiles_n, row_count, block)
    s_im = s_im.reshape(chan_count, tiles_n, row_count, block)
    z_re = jnp.einsum("ctrj,ctjm->ctrm", s_re, grid_tiles, precision=HI)
    z_im = jnp.einsum("ctrj,ctjm->ctrm", s_im, grid_tiles, precision=HI)
    place = jax.nn.one_hot(vis_block, vb_n, dtype=jnp.float32)
    r_re = jnp.einsum("ctv,ctrm->cvrm", place, z_re, precision=HI) - u_re
    r_im = jnp.einsum("ctv,ctrm->cvrm", place, z_im, precision=HI) - u_im
    sp_re = jnp.einsum("ctv,cvrm->ctrm", place, r_re, precision=HI)
    sp_im = jnp.einsum("ctv,cvrm->ctrm", place, r_im, precision=HI)
    c_re = jnp.einsum("ctrm,ctjm->ctrj", sp_re, grid_tiles, precision=HI)
    c_im = jnp.einsum("ctrm,ctjm->ctrj", sp_im, grid_tiles, precision=HI)
    c_re = c_re.reshape(flat, block)
    c_im = c_im.reshape(flat, block)
    d_re = (matmul_hi(c_re, f_cos) - matmul_hi(c_im, f_sin)) * row_scale
    d_im = (matmul_hi(c_re, f_sin) + matmul_hi(c_im, f_cos)) * row_scale
    d_re = d_re.reshape(chan_count, tiles_n, row_count, block)
    d_im = d_im.reshape(chan_count, tiles_n, row_count, block)
    dt_re = d_re * t_cos - d_im * t_sin
    dt_im = d_im * t_cos + d_re * t_sin
    return jnp.einsum("ctn,ctrm->ncrm", w_cos, dt_re, precision=HI) - jnp.einsum(
        "ctn,ctrm->ncrm", w_sin, dt_im, precision=HI
    )


def _on_device(sky_image, dual_field, sketch_matrix, grid_tiles, freq_block, vis_block, vis_data):
    chan_count, row_count, width = sky_image.shape
    block = grid_tiles.shape[2]
    blocks_n = width // block
    dual_b = lax.all_to_all(
        dual_field.reshape(blocks_n, chan_count, row_count, block), "chan", 0, 0, tiled=True
    )
    vis_all = exchange_gather(vis_data, "facet")
    sky_b = jnp.transpose(sky_image.reshape(chan_count, row_count, blocks_n, block), (2, 0, 1, 3))
    padded = padded_2(sky_b, (("facet", 2),), 1)
    grad_b = data_gradient(sky_b, grid_tiles, freq_block, vis_block, vis_all)
    smooth = 2.0 * sky_b - padded[:, :, :-2] - padded[:, :, 2:]
    new_b = sky_b - step_primal * (grad_b + smooth_weight * smooth + dual_b)
    new_image = jnp.transpose(new_b, (1, 2, 0, 3)).reshape(chan_count, row_count, width)
    rest = (1.0 - step_dual) * sky_b - 2.0 * step_dual * step_primal * (
        grad_b + smooth_weight * smooth
    )
    rest_pix = lax.all_to_all(rest, "chan", 0, 0, tiled=True).reshape(dual_field.shape)
    pixels = (1.0 - 2.0 * step_dual * step_primal) * dual_field + rest_pix
    chans = pixels.shape[0]
    flat_pix = pixels.reshape(chans, -1)
    sketch_rows = sketch_matrix.astype(jnp.float32).reshape(flat_pix.shape[1], -1)
    rank = sketch_rows.shape[1]
    part = jnp.concatenate(
        [matmul_hi(flat_pix, sketch_rows), jnp.dot(flat_pix, flat_pix.T, precision=HI)], axis=1
    )
    total = exchange_sum(part, "chan")
    sketch = total[:, :rank]
    outer = total[:, rank:]
    lower_fac = jnp.linalg.cholesky(matmul_hi(sketch.T, sketch))
    basis_mat = jax.scipy.linalg.solve_triangular(lower_fac, sketch.T, lower=True).T
    gram_mat = matmul_hi(basis_mat.T, matmul_hi(outer, basis_mat))
    shrink = shrink_matrix(gram_mat)
    coords = matmul_hi(basis_mat.T, flat_pix)
    new_dual = flat_pix - matmul_hi(matmul_hi(basis_mat, shrink), coords)
    return (new_image, new_dual.reshape(pixels.shape))


def solution(mesh):
    placed = (
        P("chan", "facet", None),
        P(None, "facet", "chan"),
        P("facet", "chan", None),
        P("chan", None, None, None),
        P("chan", None),
        P("chan", None),
        P("chan", None, "facet", None, None),
    )
    return jax.shard_map(
        _on_device,
        mesh=mesh,
        in_specs=placed,
        out_specs=(P("chan", "facet", None), P(None, "facet", "chan")),
        check_vma=False,
    )
```

```python
import math

import jax
import jax.numpy as jnp
from jax import lax
from jax.sharding import PartitionSpec as P
from jax.experimental import pallas as pl
from jax.experimental.pallas import tpu as pltpu


SIGN_ITERS = 12
ROOT_ITERS = 14


step_primal = 0.4
smooth_weight = 0.25
step_dual = 0.5
shrink_ratio = 0.25

HI = lax.Precision.HIGHEST


def padded_2(block, sides, width):
    for axis, dim in sides:
        count = lax.axis_size(axis)
        forward = [(i, i + 1) for i in range(count - 1)]
        backward = [(target, source) for source, target in forward]
        low = lax.ppermute(
            lax.slice_in_dim(block, block.shape[dim] - width, None, axis=dim), axis, forward
        )
        high = lax.ppermute(lax.slice_in_dim(block, 0, width, axis=dim), axis, backward)
        block = jnp.concatenate([low, block, high], axis=dim)
    return block


def matmul_hi(first_mat, second_mat):
    return jnp.dot(first_mat, second_mat, precision=HI)


def shrink_matrix(gram_mat):
    order_n = gram_mat.shape[0]
    identity = jnp.eye(order_n, dtype=gram_mat.dtype)
    thresh_sq = shrink_ratio * jnp.trace(gram_mat) / order_n
    shifted = gram_mat - thresh_sq * identity
    signum = shifted / jnp.sqrt(jnp.sum(shifted * shifted))

    def sign_step(turn_no, current):
        return 1.5 * current - 0.5 * matmul_hi(matmul_hi(current, current), current)

    signum = lax.fori_loop(0, SIGN_ITERS, sign_step, signum)
    keeper = 0.5 * (identity + signum)
    floored = 0.5 * (gram_mat + thresh_sq * identity + matmul_hi(shifted, signum))
    scale_c = jnp.sqrt(jnp.sum(floored * floored))

    def root_step(turn_no, stacked):
        root_iter, inv_iter = stacked[:order_n], stacked[order_n:]
        step_mat = 0.5 * (3.0 * identity - matmul_hi(inv_iter, root_iter))
        return matmul_hi(stacked, step_mat)

    stacked = lax.fori_loop(
        0, ROOT_ITERS, root_step, jnp.concatenate([floored / scale_c, identity], axis=0)
    )
    inv_iter = stacked[order_n:]
    inv_root = inv_iter / jnp.sqrt(scale_c)
    return matmul_hi(keeper, identity - jnp.sqrt(thresh_sq) * inv_root)


def _basis_kernel(gram_ref, side_ref, out_ref, work_ref, rhs_ref):
    order_n = gram_ref.shape[0]
    work_ref[...] = gram_ref[...]
    rhs_ref[...] = side_ref[...]
    lanes = lax.broadcasted_iota(jnp.int32, (1, order_n), 1)
    lanes_sq = lax.broadcasted_iota(jnp.int32, (order_n, order_n), 1)
    subs = lax.broadcasted_iota(jnp.int32, (order_n, 1), 0)

    def step(j, carry):
        row = work_ref[pl.ds(j, 1), :]
        pivot = jnp.sum(jnp.where(lanes == j, row, 0.0), axis=1, keepdims=True)
        inv_diag = 1.0 / jnp.sqrt(pivot)
        l_row = jnp.where(lanes >= j, row, 0.0) * inv_diag
        solved = rhs_ref[pl.ds(j, 1), :] * inv_diag
        out_ref[pl.ds(j, 1), :] = solved
        work = work_ref[...]
        col = jnp.sum(jnp.where(lanes_sq == j, work, 0.0), axis=1, keepdims=True)
        l_col = jnp.where(subs >= j, col, 0.0) * inv_diag
        work_ref[...] = work - l_col * l_row
        rhs_ref[...] = rhs_ref[...] - l_col * solved
        return carry

    lax.fori_loop(0, order_n, step, 0)


def basis_transposed(gram_mat, side):
    order_n = gram_mat.shape[0]
    return pl.pallas_call(
        _basis_kernel,
        out_shape=jax.ShapeDtypeStruct(side.shape, jnp.float32),
        in_specs=[pl.BlockSpec(memory_space=pltpu.VMEM)] * 2,
        out_specs=pl.BlockSpec(memory_space=pltpu.VMEM),
        scratch_shapes=[
            pltpu.VMEM(gram_mat.shape, jnp.float32),
            pltpu.VMEM(side.shape, jnp.float32),
        ],
        cost_estimate=pl.CostEstimate(
            flops=4 * order_n * order_n * (order_n + side.shape[1]),
            transcendentals=order_n,
            bytes_accessed=4 * (order_n * order_n + 2 * side.size),
        ),
    )(gram_mat, side)


def phase_of(index, period):
    angle = (2.0 * math.pi / period) * (index % period).astype(jnp.float32)
    return jnp.cos(angle), jnp.sin(angle)


def exchange_sum(value, axis):
    count = lax.axis_size(axis)
    rows = value.shape[0]
    pieces = value.reshape((count, rows // count) + value.shape[1:])
    mine = jnp.sum(lax.all_to_all(pieces, axis, 0, 0, tiled=True), axis=0)
    spread = jnp.broadcast_to(mine[None], pieces.shape)
    return lax.all_to_all(spread, axis, 0, 0, tiled=True).reshape(value.shape)


def exchange_gather(value, axis):
    count = lax.axis_size(axis)
    spread = jnp.broadcast_to(value[None], (count,) + value.shape)
    return lax.all_to_all(spread, axis, 0, 0, tiled=True)


def data_gradient(sky_b, grid_tiles, freq_block, vis_block, vis_all):
    blocks_n, chan_count, row_count, block = sky_b.shape
    width = blocks_n * block
    n_facet = vis_all.shape[0]
    all_rows = n_facet * vis_all.shape[3]
    vb_n = vis_all.shape[4]
    row0 = lax.axis_index("facet") * row_count

    p_idx = lax.broadcasted_iota(jnp.int32, (row_count, n_facet, vis_all.shape[3]), 1) * vis_all.shape[
        3
    ] + lax.broadcasted_iota(jnp.int32, (row_count, n_facet, vis_all.shape[3]), 2)
    q_idx = lax.broadcasted_iota(jnp.int32, (row_count, n_facet, vis_all.shape[3]), 0) + row0
    cos_c, sin_c = phase_of(p_idx * q_idx, all_rows)
    col_scale = 1.0 / math.sqrt(all_rows)
    v_re = vis_all[:, :, 0]
    v_im = vis_all[:, :, 1]
    u_re = (
        jnp.einsum("qfp,fcpvm->cvqm", cos_c, v_re, precision=HI)
        - jnp.einsum("qfp,fcpvm->cvqm", sin_c, v_im, precision=HI)
    ) * col_scale
    u_im = (
        jnp.einsum("qfp,fcpvm->cvqm", sin_c, v_re, precision=HI)
        + jnp.einsum("qfp,fcpvm->cvqm", cos_c, v_im, precision=HI)
    ) * col_scale

    n2_idx = lax.broadcasted_iota(jnp.int32, freq_block.shape + (blocks_n,), 2)
    w_cos, w_sin = phase_of(freq_block[:, :, None] * n2_idx, blocks_n)
    n1_idx = lax.broadcasted_iota(jnp.int32, freq_block.shape + (block,), 2)
    t_cos, t_sin = phase_of(freq_block[:, :, None] * n1_idx, width)
    t_cos = t_cos[:, :, None, :]
    t_sin = t_sin[:, :, None, :]
    j_idx = lax.broadcasted_iota(jnp.int32, (block, block), 0)
    m_idx = lax.broadcasted_iota(jnp.int32, (block, block), 1)
    f_cos, f_sin = phase_of(j_idx * m_idx, block)
    row_scale = 1.0 / math.sqrt(width)

    y_re = jnp.einsum("ctn,ncrm->ctrm", w_cos, sky_b, precision=HI)
    y_im = -jnp.einsum("ctn,ncrm->ctrm", w_sin, sky_b, precision=HI)
    yt_re = y_re * t_cos + y_im * t_sin
    yt_im = y_im * t_cos - y_re * t_sin
    tiles_n = freq_block.shape[1]
    flat = chan_count * tiles_n * row_count
    yt_re = yt_re.reshape(flat, block)
    yt_im = yt_im.reshape(flat, block)
    s_re = (matmul_hi(yt_re, f_cos) + matmul_hi(yt_im, f_sin)) * row_scale
    s_im = (matmul_hi(yt_im, f_cos) - matmul_hi(yt_re, f_sin)) * row_scale
    s_re = s_re.reshape(chan_count, tiles_n, row_count, block)
    s_im = s_im.reshape(chan_count, tiles_n, row_count, block)
    z_re = jnp.einsum("ctrj,ctjm->ctrm", s_re, grid_tiles, precision=HI)
    z_im = jnp.einsum("ctrj,ctjm->ctrm", s_im, grid_tiles, precision=HI)
    place = jax.nn.one_hot(vis_block, vb_n, dtype=jnp.float32)
    r_re = jnp.einsum("ctv,ctrm->cvrm", place, z_re, precision=HI) - u_re
    r_im = jnp.einsum("ctv,ctrm->cvrm", place, z_im, precision=HI) - u_im
    sp_re = jnp.einsum("ctv,cvrm->ctrm", place, r_re, precision=HI)
    sp_im = jnp.einsum("ctv,cvrm->ctrm", place, r_im, precision=HI)
    c_re = jnp.einsum("ctrm,ctjm->ctrj", sp_re, grid_tiles, precision=HI)
    c_im = jnp.einsum("ctrm,ctjm->ctrj", sp_im, grid_tiles, precision=HI)
    c_re = c_re.reshape(flat, block)
    c_im = c_im.reshape(flat, block)
    d_re = (matmul_hi(c_re, f_cos) - matmul_hi(c_im, f_sin)) * row_scale
    d_im = (matmul_hi(c_re, f_sin) + matmul_hi(c_im, f_cos)) * row_scale
    d_re = d_re.reshape(chan_count, tiles_n, row_count, block)
    d_im = d_im.reshape(chan_count, tiles_n, row_count, block)
    dt_re = d_re * t_cos - d_im * t_sin
    dt_im = d_im * t_cos + d_re * t_sin
    return jnp.einsum("ctn,ctrm->ncrm", w_cos, dt_re, precision=HI) - jnp.einsum(
        "ctn,ctrm->ncrm", w_sin, dt_im, precision=HI
    )


def _on_device(sky_image, dual_field, sketch_matrix, grid_tiles, freq_block, vis_block, vis_data):
    chan_count, row_count, width = sky_image.shape
    block = grid_tiles.shape[2]
    blocks_n = width // block
    dual_b = lax.all_to_all(
        dual_field.reshape(blocks_n, chan_count, row_count, block), "chan", 0, 0, tiled=True
    )
    vis_all = exchange_gather(vis_data, "facet")
    sky_b = jnp.transpose(sky_image.reshape(chan_count, row_count, blocks_n, block), (2, 0, 1, 3))
    padded = padded_2(sky_b, (("facet", 2),), 1)
    grad_b = data_gradient(sky_b, grid_tiles, freq_block, vis_block, vis_all)
    smooth = 2.0 * sky_b - padded[:, :, :-2] - padded[:, :, 2:]
    new_b = sky_b - step_primal * (grad_b + smooth_weight * smooth + dual_b)
    new_image = jnp.transpose(new_b, (1, 2, 0, 3)).reshape(chan_count, row_count, width)
    rest = (1.0 - step_dual) * sky_b - 2.0 * step_dual * step_primal * (
        grad_b + smooth_weight * smooth
    )
    rest_pix = lax.all_to_all(rest, "chan", 0, 0, tiled=True).reshape(dual_field.shape)
    pixels = (1.0 - 2.0 * step_dual * step_primal) * dual_field + rest_pix
    chans = pixels.shape[0]
    flat_pix = pixels.reshape(chans, -1)
    sketch_rows = sketch_matrix.astype(jnp.float32).reshape(flat_pix.shape[1], -1)
    rank = sketch_rows.shape[1]
    part = jnp.concatenate(
        [matmul_hi(flat_pix, sketch_rows), jnp.dot(flat_pix, flat_pix.T, precision=HI)], axis=1
    )
    total = exchange_sum(part, "chan")
    sketch = total[:, :rank]
    outer = total[:, rank:]
    basis_mat = basis_transposed(matmul_hi(sketch.T, sketch), sketch.T).T
    gram_mat = matmul_hi(basis_mat.T, matmul_hi(outer, basis_mat))
    shrink = shrink_matrix(gram_mat)
    coords = matmul_hi(basis_mat.T, flat_pix)
    new_dual = flat_pix - matmul_hi(matmul_hi(basis_mat, shrink), coords)
    return (new_image, new_dual.reshape(pixels.shape))


def solution(mesh):
    placed = (
        P("chan", "facet", None),
        P(None, "facet", "chan"),
        P("facet", "chan", None),
        P("chan", None, None, None),
        P("chan", None),
        P("chan", None),
        P("chan", None, "facet", None, None),
    )
    return jax.shard_map(
        _on_device,
        mesh=mesh,
        in_specs=placed,
        out_specs=(P("chan", "facet", None), P(None, "facet", "chan")),
        check_vma=False,
    )
```

```python
import math

import jax
import jax.numpy as jnp
from jax import lax
from jax.sharding import PartitionSpec as P
from jax.experimental import pallas as pl
from jax.experimental.pallas import tpu as pltpu


SIGN_ITERS = 12
ROOT_ITERS = 14


step_primal = 0.4
smooth_weight = 0.25
step_dual = 0.5
shrink_ratio = 0.25

HI = lax.Precision.HIGHEST


def padded_2(block, sides, width):
    for axis, dim in sides:
        count = lax.axis_size(axis)
        forward = [(i, i + 1) for i in range(count - 1)]
        backward = [(target, source) for source, target in forward]
        low = lax.ppermute(
            lax.slice_in_dim(block, block.shape[dim] - width, None, axis=dim), axis, forward
        )
        high = lax.ppermute(lax.slice_in_dim(block, 0, width, axis=dim), axis, backward)
        block = jnp.concatenate([low, block, high], axis=dim)
    return block


def matmul_hi(first_mat, second_mat):
    return jnp.dot(first_mat, second_mat, precision=HI)


def shrink_matrix(gram_mat):
    order_n = gram_mat.shape[0]
    identity = jnp.eye(order_n, dtype=gram_mat.dtype)
    thresh_sq = shrink_ratio * jnp.trace(gram_mat) / order_n
    shifted = gram_mat - thresh_sq * identity
    signum = shifted / jnp.sqrt(jnp.sum(shifted * shifted))

    def sign_step(turn_no, current):
        return 1.5 * current - 0.5 * matmul_hi(matmul_hi(current, current), current)

    signum = lax.fori_loop(0, SIGN_ITERS, sign_step, signum)
    keeper = 0.5 * (identity + signum)
    floored = 0.5 * (gram_mat + thresh_sq * identity + matmul_hi(shifted, signum))
    scale_c = jnp.sqrt(jnp.sum(floored * floored))

    def root_step(turn_no, stacked):
        root_iter, inv_iter = stacked[:order_n], stacked[order_n:]
        step_mat = 0.5 * (3.0 * identity - matmul_hi(inv_iter, root_iter))
        return matmul_hi(stacked, step_mat)

    stacked = lax.fori_loop(
        0, ROOT_ITERS, root_step, jnp.concatenate([floored / scale_c, identity], axis=0)
    )
    inv_iter = stacked[order_n:]
    inv_root = inv_iter / jnp.sqrt(scale_c)
    return matmul_hi(keeper, identity - jnp.sqrt(thresh_sq) * inv_root)


def _basis_kernel(gram_ref, side_ref, out_ref, work_ref, rhs_ref):
    order_n = gram_ref.shape[0]
    work_ref[...] = gram_ref[...]
    rhs_ref[...] = side_ref[...]
    lanes = lax.broadcasted_iota(jnp.int32, (1, order_n), 1)
    lanes_sq = lax.broadcasted_iota(jnp.int32, (order_n, order_n), 1)
    subs = lax.broadcasted_iota(jnp.int32, (order_n, 1), 0)

    def pick(vec, k):
        return jnp.sum(jnp.where(lanes == k, vec, 0.0), axis=1, keepdims=True)

    def step(t, carry):
        j = 2 * t
        row0 = work_ref[pl.ds(j, 1), :]
        row1 = work_ref[pl.ds(j + 1, 1), :]
        diag0 = jnp.sqrt(pick(row0, j))
        low10 = pick(row0, j + 1) / diag0
        diag1 = jnp.sqrt(pick(row1, j + 1) - low10 * low10)
        l_row0 = jnp.where(lanes >= j, row0, 0.0) / diag0
        l_row1 = jnp.where(lanes >= j + 1, row1 - l_row0 * low10, 0.0) / diag1
        work = work_ref[...]
        col0 = jnp.sum(jnp.where(lanes_sq == j, work, 0.0), axis=1, keepdims=True)
        col1 = jnp.sum(jnp.where(lanes_sq == j + 1, work, 0.0), axis=1, keepdims=True)
        l_col0 = jnp.where(subs >= j, col0, 0.0) / diag0
        l_col1 = jnp.where(subs >= j + 1, col1 - l_col0 * low10, 0.0) / diag1
        solved0 = rhs_ref[pl.ds(j, 1), :] / diag0
        solved1 = (rhs_ref[pl.ds(j + 1, 1), :] - low10 * solved0) / diag1
        out_ref[pl.ds(j, 1), :] = solved0
        out_ref[pl.ds(j + 1, 1), :] = solved1
        work_ref[...] = work - l_col0 * l_row0 - l_col1 * l_row1
        rhs_ref[...] = rhs_ref[...] - l_col0 * solved0 - l_col1 * solved1
        return carry

    lax.fori_loop(0, order_n // 2, step, 0)


def basis_transposed(gram_mat, side):
    order_n = gram_mat.shape[0]
    return pl.pallas_call(
        _basis_kernel,
        out_shape=jax.ShapeDtypeStruct(side.shape, jnp.float32),
        in_specs=[pl.BlockSpec(memory_space=pltpu.VMEM)] * 2,
        out_specs=pl.BlockSpec(memory_space=pltpu.VMEM),
        scratch_shapes=[
            pltpu.VMEM(gram_mat.shape, jnp.float32),
            pltpu.VMEM(side.shape, jnp.float32),
        ],
        cost_estimate=pl.CostEstimate(
            flops=4 * order_n * order_n * (order_n + side.shape[1]),
            transcendentals=order_n,
            bytes_accessed=4 * (order_n * order_n + 2 * side.size),
        ),
    )(gram_mat, side)


def phase_of(index, period):
    angle = (2.0 * math.pi / period) * (index % period).astype(jnp.float32)
    return jnp.cos(angle), jnp.sin(angle)


def exchange_sum(value, axis):
    count = lax.axis_size(axis)
    rows = value.shape[0]
    pieces = value.reshape((count, rows // count) + value.shape[1:])
    mine = jnp.sum(lax.all_to_all(pieces, axis, 0, 0, tiled=True), axis=0)
    spread = jnp.broadcast_to(mine[None], pieces.shape)
    return lax.all_to_all(spread, axis, 0, 0, tiled=True).reshape(value.shape)


def exchange_gather(value, axis):
    count = lax.axis_size(axis)
    spread = jnp.broadcast_to(value[None], (count,) + value.shape)
    return lax.all_to_all(spread, axis, 0, 0, tiled=True)


def data_gradient(sky_b, grid_tiles, freq_block, vis_block, vis_all):
    blocks_n, chan_count, row_count, block = sky_b.shape
    width = blocks_n * block
    n_facet = vis_all.shape[0]
    all_rows = n_facet * vis_all.shape[3]
    vb_n = vis_all.shape[4]
    row0 = lax.axis_index("facet") * row_count

    p_idx = lax.broadcasted_iota(jnp.int32, (row_count, n_facet, vis_all.shape[3]), 1) * vis_all.shape[
        3
    ] + lax.broadcasted_iota(jnp.int32, (row_count, n_facet, vis_all.shape[3]), 2)
    q_idx = lax.broadcasted_iota(jnp.int32, (row_count, n_facet, vis_all.shape[3]), 0) + row0
    cos_c, sin_c = phase_of(p_idx * q_idx, all_rows)
    col_scale = 1.0 / math.sqrt(all_rows)
    v_re = vis_all[:, :, 0]
    v_im = vis_all[:, :, 1]
    u_re = (
        jnp.einsum("qfp,fcpvm->cvqm", cos_c, v_re, precision=HI)
        - jnp.einsum("qfp,fcpvm->cvqm", sin_c, v_im, precision=HI)
    ) * col_scale
    u_im = (
        jnp.einsum("qfp,fcpvm->cvqm", sin_c, v_re, precision=HI)
        + jnp.einsum("qfp,fcpvm->cvqm", cos_c, v_im, precision=HI)
    ) * col_scale

    n2_idx = lax.broadcasted_iota(jnp.int32, freq_block.shape + (blocks_n,), 2)
    w_cos, w_sin = phase_of(freq_block[:, :, None] * n2_idx, blocks_n)
    n1_idx = lax.broadcasted_iota(jnp.int32, freq_block.shape + (block,), 2)
    t_cos, t_sin = phase_of(freq_block[:, :, None] * n1_idx, width)
    t_cos = t_cos[:, :, None, :]
    t_sin = t_sin[:, :, None, :]
    j_idx = lax.broadcasted_iota(jnp.int32, (block, block), 0)
    m_idx = lax.broadcasted_iota(jnp.int32, (block, block), 1)
    f_cos, f_sin = phase_of(j_idx * m_idx, block)
    row_scale = 1.0 / math.sqrt(width)

    y_re = jnp.einsum("ctn,ncrm->ctrm", w_cos, sky_b, precision=HI)
    y_im = -jnp.einsum("ctn,ncrm->ctrm", w_sin, sky_b, precision=HI)
    yt_re = y_re * t_cos + y_im * t_sin
    yt_im = y_im * t_cos - y_re * t_sin
    tiles_n = freq_block.shape[1]
    flat = chan_count * tiles_n * row_count
    yt_re = yt_re.reshape(flat, block)
    yt_im = yt_im.reshape(flat, block)
    s_re = (matmul_hi(yt_re, f_cos) + matmul_hi(yt_im, f_sin)) * row_scale
    s_im = (matmul_hi(yt_im, f_cos) - matmul_hi(yt_re, f_sin)) * row_scale
    s_re = s_re.reshape(chan_count, tiles_n, row_count, block)
    s_im = s_im.reshape(chan_count, tiles_n, row_count, block)
    z_re = jnp.einsum("ctrj,ctjm->ctrm", s_re, grid_tiles, precision=HI)
    z_im = jnp.einsum("ctrj,ctjm->ctrm", s_im, grid_tiles, precision=HI)
    place = jax.nn.one_hot(vis_block, vb_n, dtype=jnp.float32)
    r_re = jnp.einsum("ctv,ctrm->cvrm", place, z_re, precision=HI) - u_re
    r_im = jnp.einsum("ctv,ctrm->cvrm", place, z_im, precision=HI) - u_im
    sp_re = jnp.einsum("ctv,cvrm->ctrm", place, r_re, precision=HI)
    sp_im = jnp.einsum("ctv,cvrm->ctrm", place, r_im, precision=HI)
    c_re = jnp.einsum("ctrm,ctjm->ctrj", sp_re, grid_tiles, precision=HI)
    c_im = jnp.einsum("ctrm,ctjm->ctrj", sp_im, grid_tiles, precision=HI)
    c_re = c_re.reshape(flat, block)
    c_im = c_im.reshape(flat, block)
    d_re = (matmul_hi(c_re, f_cos) - matmul_hi(c_im, f_sin)) * row_scale
    d_im = (matmul_hi(c_re, f_sin) + matmul_hi(c_im, f_cos)) * row_scale
    d_re = d_re.reshape(chan_count, tiles_n, row_count, block)
    d_im = d_im.reshape(chan_count, tiles_n, row_count, block)
    dt_re = d_re * t_cos - d_im * t_sin
    dt_im = d_im * t_cos + d_re * t_sin
    return jnp.einsum("ctn,ctrm->ncrm", w_cos, dt_re, precision=HI) - jnp.einsum(
        "ctn,ctrm->ncrm", w_sin, dt_im, precision=HI
    )


def _on_device(sky_image, dual_field, sketch_matrix, grid_tiles, freq_block, vis_block, vis_data):
    chan_count, row_count, width = sky_image.shape
    block = grid_tiles.shape[2]
    blocks_n = width // block
    dual_b = lax.all_to_all(
        dual_field.reshape(blocks_n, chan_count, row_count, block), "chan", 0, 0, tiled=True
    )
    vis_all = exchange_gather(vis_data, "facet")
    sky_b = jnp.transpose(sky_image.reshape(chan_count, row_count, blocks_n, block), (2, 0, 1, 3))
    padded = padded_2(sky_b, (("facet", 2),), 1)
    grad_b = data_gradient(sky_b, grid_tiles, freq_block, vis_block, vis_all)
    smooth = 2.0 * sky_b - padded[:, :, :-2] - padded[:, :, 2:]
    new_b = sky_b - step_primal * (grad_b + smooth_weight * smooth + dual_b)
    new_image = jnp.transpose(new_b, (1, 2, 0, 3)).reshape(chan_count, row_count, width)
    rest = (1.0 - step_dual) * sky_b - 2.0 * step_dual * step_primal * (
        grad_b + smooth_weight * smooth
    )
    rest_pix = lax.all_to_all(rest, "chan", 0, 0, tiled=True).reshape(dual_field.shape)
    pixels = (1.0 - 2.0 * step_dual * step_primal) * dual_field + rest_pix
    chans = pixels.shape[0]
    flat_pix = pixels.reshape(chans, -1)
    sketch_rows = sketch_matrix.astype(jnp.float32).reshape(flat_pix.shape[1], -1)
    rank = sketch_rows.shape[1]
    part = jnp.concatenate(
        [matmul_hi(flat_pix, sketch_rows), jnp.dot(flat_pix, flat_pix.T, precision=HI)], axis=1
    )
    total = exchange_sum(part, "chan")
    sketch = total[:, :rank]
    outer = total[:, rank:]
    basis_mat = basis_transposed(matmul_hi(sketch.T, sketch), sketch.T).T
    gram_mat = matmul_hi(basis_mat.T, matmul_hi(outer, basis_mat))
    shrink = shrink_matrix(gram_mat)
    coords = matmul_hi(basis_mat.T, flat_pix)
    new_dual = flat_pix - matmul_hi(matmul_hi(basis_mat, shrink), coords)
    return (new_image, new_dual.reshape(pixels.shape))


def solution(mesh):
    placed = (
        P("chan", "facet", None),
        P(None, "facet", "chan"),
        P("facet", "chan", None),
        P("chan", None, None, None),
        P("chan", None),
        P("chan", None),
        P("chan", None, "facet", None, None),
    )
    return jax.shard_map(
        _on_device,
        mesh=mesh,
        in_specs=placed,
        out_specs=(P("chan", "facet", None), P(None, "facet", "chan")),
        check_vma=False,
    )
```

```python
import math

import jax
import jax.numpy as jnp
from jax import lax
from jax.sharding import PartitionSpec as P
from jax.experimental import pallas as pl
from jax.experimental.pallas import tpu as pltpu


SIGN_ITERS = 12
ROOT_ITERS = 14


step_primal = 0.4
smooth_weight = 0.25
step_dual = 0.5
shrink_ratio = 0.25

HI = lax.Precision.HIGHEST


def padded_2(block, sides, width):
    for axis, dim in sides:
        count = lax.axis_size(axis)
        forward = [(i, i + 1) for i in range(count - 1)]
        backward = [(target, source) for source, target in forward]
        low = lax.ppermute(
            lax.slice_in_dim(block, block.shape[dim] - width, None, axis=dim), axis, forward
        )
        high = lax.ppermute(lax.slice_in_dim(block, 0, width, axis=dim), axis, backward)
        block = jnp.concatenate([low, block, high], axis=dim)
    return block


def matmul_hi(first_mat, second_mat):
    return jnp.dot(first_mat, second_mat, precision=HI)


def shrink_matrix(gram_mat):
    order_n = gram_mat.shape[0]
    identity = jnp.eye(order_n, dtype=gram_mat.dtype)
    thresh_sq = shrink_ratio * jnp.trace(gram_mat) / order_n
    shifted = gram_mat - thresh_sq * identity
    signum = shifted / jnp.sqrt(jnp.sum(shifted * shifted))

    def iter_mm(first_mat, second_mat):
        return jnp.dot(first_mat, second_mat, precision=lax.Precision.HIGH)

    def sign_step(turn_no, current):
        return 1.5 * current - 0.5 * iter_mm(iter_mm(current, current), current)

    signum = lax.fori_loop(0, SIGN_ITERS, sign_step, signum)
    keeper = 0.5 * (identity + signum)
    floored = 0.5 * (gram_mat + thresh_sq * identity + matmul_hi(shifted, signum))
    scale_c = jnp.sqrt(jnp.sum(floored * floored))

    def root_step(turn_no, stacked):
        root_iter, inv_iter = stacked[:order_n], stacked[order_n:]
        step_mat = 0.5 * (3.0 * identity - iter_mm(inv_iter, root_iter))
        return iter_mm(stacked, step_mat)

    stacked = lax.fori_loop(
        0, ROOT_ITERS, root_step, jnp.concatenate([floored / scale_c, identity], axis=0)
    )
    inv_iter = stacked[order_n:]
    inv_root = inv_iter / jnp.sqrt(scale_c)
    return matmul_hi(keeper, identity - jnp.sqrt(thresh_sq) * inv_root)


def _basis_kernel(gram_ref, side_ref, out_ref, work_ref, rhs_ref):
    order_n = gram_ref.shape[0]
    work_ref[...] = gram_ref[...]
    rhs_ref[...] = side_ref[...]
    lanes = lax.broadcasted_iota(jnp.int32, (1, order_n), 1)
    lanes_sq = lax.broadcasted_iota(jnp.int32, (order_n, order_n), 1)
    subs = lax.broadcasted_iota(jnp.int32, (order_n, 1), 0)

    def pick(vec, k):
        return jnp.sum(jnp.where(lanes == k, vec, 0.0), axis=1, keepdims=True)

    def step(t, carry):
        j = 2 * t
        row0 = work_ref[pl.ds(j, 1), :]
        row1 = work_ref[pl.ds(j + 1, 1), :]
        diag0 = jnp.sqrt(pick(row0, j))
        low10 = pick(row0, j + 1) / diag0
        diag1 = jnp.sqrt(pick(row1, j + 1) - low10 * low10)
        l_row0 = jnp.where(lanes >= j, row0, 0.0) / diag0
        l_row1 = jnp.where(lanes >= j + 1, row1 - l_row0 * low10, 0.0) / diag1
        work = work_ref[...]
        col0 = jnp.sum(jnp.where(lanes_sq == j, work, 0.0), axis=1, keepdims=True)
        col1 = jnp.sum(jnp.where(lanes_sq == j + 1, work, 0.0), axis=1, keepdims=True)
        l_col0 = jnp.where(subs >= j, col0, 0.0) / diag0
        l_col1 = jnp.where(subs >= j + 1, col1 - l_col0 * low10, 0.0) / diag1
        solved0 = rhs_ref[pl.ds(j, 1), :] / diag0
        solved1 = (rhs_ref[pl.ds(j + 1, 1), :] - low10 * solved0) / diag1
        out_ref[pl.ds(j, 1), :] = solved0
        out_ref[pl.ds(j + 1, 1), :] = solved1
        work_ref[...] = work - l_col0 * l_row0 - l_col1 * l_row1
        rhs_ref[...] = rhs_ref[...] - l_col0 * solved0 - l_col1 * solved1
        return carry

    lax.fori_loop(0, order_n // 2, step, 0)


def basis_transposed(gram_mat, side):
    order_n = gram_mat.shape[0]
    return pl.pallas_call(
        _basis_kernel,
        out_shape=jax.ShapeDtypeStruct(side.shape, jnp.float32),
        in_specs=[pl.BlockSpec(memory_space=pltpu.VMEM)] * 2,
        out_specs=pl.BlockSpec(memory_space=pltpu.VMEM),
        scratch_shapes=[
            pltpu.VMEM(gram_mat.shape, jnp.float32),
            pltpu.VMEM(side.shape, jnp.float32),
        ],
        cost_estimate=pl.CostEstimate(
            flops=4 * order_n * order_n * (order_n + side.shape[1]),
            transcendentals=order_n,
            bytes_accessed=4 * (order_n * order_n + 2 * side.size),
        ),
    )(gram_mat, side)


def phase_of(index, period):
    angle = (2.0 * math.pi / period) * (index % period).astype(jnp.float32)
    return jnp.cos(angle), jnp.sin(angle)


def exchange_sum(value, axis):
    count = lax.axis_size(axis)
    rows = value.shape[0]
    pieces = value.reshape((count, rows // count) + value.shape[1:])
    mine = jnp.sum(lax.all_to_all(pieces, axis, 0, 0, tiled=True), axis=0)
    spread = jnp.broadcast_to(mine[None], pieces.shape)
    return lax.all_to_all(spread, axis, 0, 0, tiled=True).reshape(value.shape)


def data_gradient(sky_b, grid_tiles, freq_block, vis_block, vis_all):
    blocks_n, chan_count, row_count, block = sky_b.shape
    width = blocks_n * block
    n_facet = vis_all.shape[0]
    all_rows = n_facet * vis_all.shape[3]
    vb_n = vis_all.shape[4]
    row0 = lax.axis_index("facet") * row_count

    p_idx = lax.broadcasted_iota(jnp.int32, (row_count, n_facet, vis_all.shape[3]), 1) * vis_all.shape[
        3
    ] + lax.broadcasted_iota(jnp.int32, (row_count, n_facet, vis_all.shape[3]), 2)
    q_idx = lax.broadcasted_iota(jnp.int32, (row_count, n_facet, vis_all.shape[3]), 0) + row0
    cos_c, sin_c = phase_of(p_idx * q_idx, all_rows)
    col_scale = 1.0 / math.sqrt(all_rows)
    v_re = vis_all[:, :, 0]
    v_im = vis_all[:, :, 1]
    u_re = (
        jnp.einsum("qfp,fcpvm->cvqm", cos_c, v_re, precision=HI)
        - jnp.einsum("qfp,fcpvm->cvqm", sin_c, v_im, precision=HI)
    ) * col_scale
    u_im = (
        jnp.einsum("qfp,fcpvm->cvqm", sin_c, v_re, precision=HI)
        + jnp.einsum("qfp,fcpvm->cvqm", cos_c, v_im, precision=HI)
    ) * col_scale

    n2_idx = lax.broadcasted_iota(jnp.int32, freq_block.shape + (blocks_n,), 2)
    w_cos, w_sin = phase_of(freq_block[:, :, None] * n2_idx, blocks_n)
    n1_idx = lax.broadcasted_iota(jnp.int32, freq_block.shape + (block,), 2)
    t_cos, t_sin = phase_of(freq_block[:, :, None] * n1_idx, width)
    t_cos = t_cos[:, :, None, :]
    t_sin = t_sin[:, :, None, :]
    j_idx = lax.broadcasted_iota(jnp.int32, (block, block), 0)
    m_idx = lax.broadcasted_iota(jnp.int32, (block, block), 1)
    f_cos, f_sin = phase_of(j_idx * m_idx, block)
    row_scale = 1.0 / math.sqrt(width)

    y_re = jnp.einsum("ctn,ncrm->ctrm", w_cos, sky_b, precision=HI)
    y_im = -jnp.einsum("ctn,ncrm->ctrm", w_sin, sky_b, precision=HI)
    yt_re = y_re * t_cos + y_im * t_sin
    yt_im = y_im * t_cos - y_re * t_sin
    tiles_n = freq_block.shape[1]
    flat = chan_count * tiles_n * row_count
    yt_re = yt_re.reshape(flat, block)
    yt_im = yt_im.reshape(flat, block)
    s_re = (matmul_hi(yt_re, f_cos) + matmul_hi(yt_im, f_sin)) * row_scale
    s_im = (matmul_hi(yt_im, f_cos) - matmul_hi(yt_re, f_sin)) * row_scale
    s_re = s_re.reshape(chan_count, tiles_n, row_count, block)
    s_im = s_im.reshape(chan_count, tiles_n, row_count, block)
    z_re = jnp.einsum("ctrj,ctjm->ctrm", s_re, grid_tiles, precision=HI)
    z_im = jnp.einsum("ctrj,ctjm->ctrm", s_im, grid_tiles, precision=HI)
    place = jax.nn.one_hot(vis_block, vb_n, dtype=jnp.float32)
    r_re = jnp.einsum("ctv,ctrm->cvrm", place, z_re, precision=HI) - u_re
    r_im = jnp.einsum("ctv,ctrm->cvrm", place, z_im, precision=HI) - u_im
    sp_re = jnp.einsum("ctv,cvrm->ctrm", place, r_re, precision=HI)
    sp_im = jnp.einsum("ctv,cvrm->ctrm", place, r_im, precision=HI)
    c_re = jnp.einsum("ctrm,ctjm->ctrj", sp_re, grid_tiles, precision=HI)
    c_im = jnp.einsum("ctrm,ctjm->ctrj", sp_im, grid_tiles, precision=HI)
    c_re = c_re.reshape(flat, block)
    c_im = c_im.reshape(flat, block)
    d_re = (matmul_hi(c_re, f_cos) - matmul_hi(c_im, f_sin)) * row_scale
    d_im = (matmul_hi(c_re, f_sin) + matmul_hi(c_im, f_cos)) * row_scale
    d_re = d_re.reshape(chan_count, tiles_n, row_count, block)
    d_im = d_im.reshape(chan_count, tiles_n, row_count, block)
    dt_re = d_re * t_cos - d_im * t_sin
    dt_im = d_im * t_cos + d_re * t_sin
    return jnp.einsum("ctn,ctrm->ncrm", w_cos, dt_re, precision=HI) - jnp.einsum(
        "ctn,ctrm->ncrm", w_sin, dt_im, precision=HI
    )


def _on_device(sky_image, dual_field, sketch_matrix, grid_tiles, freq_block, vis_block, vis_data):
    chan_count, row_count, width = sky_image.shape
    block = grid_tiles.shape[2]
    blocks_n = width // block
    dual_b = lax.all_to_all(
        dual_field.reshape(blocks_n, chan_count, row_count, block), "chan", 0, 0, tiled=True
    )
    vis_all = lax.all_gather(vis_data, "facet", axis=0)
    sky_b = jnp.transpose(sky_image.reshape(chan_count, row_count, blocks_n, block), (2, 0, 1, 3))
    padded = padded_2(sky_b, (("facet", 2),), 1)
    grad_b = data_gradient(sky_b, grid_tiles, freq_block, vis_block, vis_all)
    smooth = 2.0 * sky_b - padded[:, :, :-2] - padded[:, :, 2:]
    new_b = sky_b - step_primal * (grad_b + smooth_weight * smooth + dual_b)
    new_image = jnp.transpose(new_b, (1, 2, 0, 3)).reshape(chan_count, row_count, width)
    rest = (1.0 - step_dual) * sky_b - 2.0 * step_dual * step_primal * (
        grad_b + smooth_weight * smooth
    )
    rest_pix = lax.all_to_all(rest, "chan", 0, 0, tiled=True).reshape(dual_field.shape)
    pixels = (1.0 - 2.0 * step_dual * step_primal) * dual_field + rest_pix
    chans = pixels.shape[0]
    flat_pix = pixels.reshape(chans, -1)
    sketch_rows = sketch_matrix.astype(jnp.float32).reshape(flat_pix.shape[1], -1)
    rank = sketch_rows.shape[1]
    part = jnp.concatenate(
        [matmul_hi(flat_pix, sketch_rows), jnp.dot(flat_pix, flat_pix.T, precision=HI)], axis=1
    )
    total = exchange_sum(part, "chan")
    sketch = total[:, :rank]
    outer = total[:, rank:]
    basis_mat = basis_transposed(matmul_hi(sketch.T, sketch), sketch.T).T
    gram_mat = matmul_hi(basis_mat.T, matmul_hi(outer, basis_mat))
    shrink = shrink_matrix(gram_mat)
    coords = matmul_hi(basis_mat.T, flat_pix)
    new_dual = flat_pix - matmul_hi(matmul_hi(basis_mat, shrink), coords)
    return (new_image, new_dual.reshape(pixels.shape))


def solution(mesh):
    placed = (
        P("chan", "facet", None),
        P(None, "facet", "chan"),
        P("facet", "chan", None),
        P("chan", None, None, None),
        P("chan", None),
        P("chan", None),
        P("chan", None, "facet", None, None),
    )
    return jax.shard_map(
        _on_device,
        mesh=mesh,
        in_specs=placed,
        out_specs=(P("chan", "facet", None), P(None, "facet", "chan")),
        check_vma=False,
    )
```

```python
import math

import jax
import jax.numpy as jnp
from jax import lax
from jax.sharding import PartitionSpec as P
from jax.experimental import pallas as pl
from jax.experimental.pallas import tpu as pltpu


SIGN_ITERS = 12
ROOT_ITERS = 14


step_primal = 0.4
smooth_weight = 0.25
step_dual = 0.5
shrink_ratio = 0.25

HI = lax.Precision.HIGHEST


def padded_2(block, sides, width):
    for axis, dim in sides:
        count = lax.axis_size(axis)
        forward = [(i, i + 1) for i in range(count - 1)]
        backward = [(target, source) for source, target in forward]
        low = lax.ppermute(
            lax.slice_in_dim(block, block.shape[dim] - width, None, axis=dim), axis, forward
        )
        high = lax.ppermute(lax.slice_in_dim(block, 0, width, axis=dim), axis, backward)
        block = jnp.concatenate([low, block, high], axis=dim)
    return block


def matmul_hi(first_mat, second_mat):
    return jnp.dot(first_mat, second_mat, precision=HI)


def shrink_matrix(gram_mat):
    order_n = gram_mat.shape[0]
    identity = jnp.eye(order_n, dtype=gram_mat.dtype)
    thresh_sq = shrink_ratio * jnp.trace(gram_mat) / order_n
    shifted = gram_mat - thresh_sq * identity
    signum = shifted / jnp.sqrt(jnp.sum(shifted * shifted))

    def iter_mm(first_mat, second_mat):
        return jnp.dot(first_mat, second_mat, precision=lax.Precision.HIGH)

    def sign_step(turn_no, current):
        return 1.5 * current - 0.5 * iter_mm(iter_mm(current, current), current)

    signum = lax.fori_loop(0, SIGN_ITERS, sign_step, signum, unroll=True)
    keeper = 0.5 * (identity + signum)
    floored = 0.5 * (gram_mat + thresh_sq * identity + matmul_hi(shifted, signum))
    scale_c = jnp.sqrt(jnp.sum(floored * floored))

    def root_step(turn_no, stacked):
        root_iter, inv_iter = stacked[:order_n], stacked[order_n:]
        step_mat = 0.5 * (3.0 * identity - iter_mm(inv_iter, root_iter))
        return iter_mm(stacked, step_mat)

    stacked = lax.fori_loop(
        0, ROOT_ITERS, root_step, jnp.concatenate([floored / scale_c, identity], axis=0), unroll=True
    )
    inv_iter = stacked[order_n:]
    inv_root = inv_iter / jnp.sqrt(scale_c)
    return matmul_hi(keeper, identity - jnp.sqrt(thresh_sq) * inv_root)


def _basis_kernel(gram_ref, side_ref, out_ref, work_ref, rhs_ref):
    order_n = gram_ref.shape[0]
    work_ref[...] = gram_ref[...]
    rhs_ref[...] = side_ref[...]
    lanes = lax.broadcasted_iota(jnp.int32, (1, order_n), 1)
    lanes_sq = lax.broadcasted_iota(jnp.int32, (order_n, order_n), 1)
    subs = lax.broadcasted_iota(jnp.int32, (order_n, 1), 0)

    def pick(vec, k):
        return jnp.sum(jnp.where(lanes == k, vec, 0.0), axis=1, keepdims=True)

    def step(t, carry):
        j = 2 * t
        row0 = work_ref[pl.ds(j, 1), :]
        row1 = work_ref[pl.ds(j + 1, 1), :]
        diag0 = jnp.sqrt(pick(row0, j))
        low10 = pick(row0, j + 1) / diag0
        diag1 = jnp.sqrt(pick(row1, j + 1) - low10 * low10)
        l_row0 = jnp.where(lanes >= j, row0, 0.0) / diag0
        l_row1 = jnp.where(lanes >= j + 1, row1 - l_row0 * low10, 0.0) / diag1
        work = work_ref[...]
        col0 = jnp.sum(jnp.where(lanes_sq == j, work, 0.0), axis=1, keepdims=True)
        col1 = jnp.sum(jnp.where(lanes_sq == j + 1, work, 0.0), axis=1, keepdims=True)
        l_col0 = jnp.where(subs >= j, col0, 0.0) / diag0
        l_col1 = jnp.where(subs >= j + 1, col1 - l_col0 * low10, 0.0) / diag1
        solved0 = rhs_ref[pl.ds(j, 1), :] / diag0
        solved1 = (rhs_ref[pl.ds(j + 1, 1), :] - low10 * solved0) / diag1
        out_ref[pl.ds(j, 1), :] = solved0
        out_ref[pl.ds(j + 1, 1), :] = solved1
        work_ref[...] = work - l_col0 * l_row0 - l_col1 * l_row1
        rhs_ref[...] = rhs_ref[...] - l_col0 * solved0 - l_col1 * solved1
        return carry

    lax.fori_loop(0, order_n // 2, step, 0)


def basis_transposed(gram_mat, side):
    order_n = gram_mat.shape[0]
    return pl.pallas_call(
        _basis_kernel,
        out_shape=jax.ShapeDtypeStruct(side.shape, jnp.float32),
        in_specs=[pl.BlockSpec(memory_space=pltpu.VMEM)] * 2,
        out_specs=pl.BlockSpec(memory_space=pltpu.VMEM),
        scratch_shapes=[
            pltpu.VMEM(gram_mat.shape, jnp.float32),
            pltpu.VMEM(side.shape, jnp.float32),
        ],
        cost_estimate=pl.CostEstimate(
            flops=4 * order_n * order_n * (order_n + side.shape[1]),
            transcendentals=order_n,
            bytes_accessed=4 * (order_n * order_n + 2 * side.size),
        ),
    )(gram_mat, side)


def phase_of(index, period):
    angle = (2.0 * math.pi / period) * (index % period).astype(jnp.float32)
    return jnp.cos(angle), jnp.sin(angle)


def exchange_sum(value, axis):
    count = lax.axis_size(axis)
    rows = value.shape[0]
    pieces = value.reshape((count, rows // count) + value.shape[1:])
    mine = jnp.sum(lax.all_to_all(pieces, axis, 0, 0, tiled=True), axis=0)
    spread = jnp.broadcast_to(mine[None], pieces.shape)
    return lax.all_to_all(spread, axis, 0, 0, tiled=True).reshape(value.shape)


def exchange_gather(value, axis):
    count = lax.axis_size(axis)
    spread = jnp.broadcast_to(value[None], (count,) + value.shape)
    return lax.all_to_all(spread, axis, 0, 0, tiled=True)


def data_gradient(sky_b, grid_tiles, freq_block, vis_block, vis_all):
    blocks_n, chan_count, row_count, block = sky_b.shape
    width = blocks_n * block
    n_facet = vis_all.shape[0]
    all_rows = n_facet * vis_all.shape[3]
    vb_n = vis_all.shape[4]
    row0 = lax.axis_index("facet") * row_count

    p_idx = lax.broadcasted_iota(jnp.int32, (row_count, n_facet, vis_all.shape[3]), 1) * vis_all.shape[
        3
    ] + lax.broadcasted_iota(jnp.int32, (row_count, n_facet, vis_all.shape[3]), 2)
    q_idx = lax.broadcasted_iota(jnp.int32, (row_count, n_facet, vis_all.shape[3]), 0) + row0
    cos_c, sin_c = phase_of(p_idx * q_idx, all_rows)
    col_scale = 1.0 / math.sqrt(all_rows)
    v_re = vis_all[:, :, 0]
    v_im = vis_all[:, :, 1]
    u_re = (
        jnp.einsum("qfp,fcpvm->cvqm", cos_c, v_re, precision=HI)
        - jnp.einsum("qfp,fcpvm->cvqm", sin_c, v_im, precision=HI)
    ) * col_scale
    u_im = (
        jnp.einsum("qfp,fcpvm->cvqm", sin_c, v_re, precision=HI)
        + jnp.einsum("qfp,fcpvm->cvqm", cos_c, v_im, precision=HI)
    ) * col_scale

    n2_idx = lax.broadcasted_iota(jnp.int32, freq_block.shape + (blocks_n,), 2)
    w_cos, w_sin = phase_of(freq_block[:, :, None] * n2_idx, blocks_n)
    n1_idx = lax.broadcasted_iota(jnp.int32, freq_block.shape + (block,), 2)
    t_cos, t_sin = phase_of(freq_block[:, :, None] * n1_idx, width)
    t_cos = t_cos[:, :, None, :]
    t_sin = t_sin[:, :, None, :]
    j_idx = lax.broadcasted_iota(jnp.int32, (block, block), 0)
    m_idx = lax.broadcasted_iota(jnp.int32, (block, block), 1)
    f_cos, f_sin = phase_of(j_idx * m_idx, block)
    row_scale = 1.0 / math.sqrt(width)

    y_re = jnp.einsum("ctn,ncrm->ctrm", w_cos, sky_b, precision=HI)
    y_im = -jnp.einsum("ctn,ncrm->ctrm", w_sin, sky_b, precision=HI)
    yt_re = y_re * t_cos + y_im * t_sin
    yt_im = y_im * t_cos - y_re * t_sin
    tiles_n = freq_block.shape[1]
    flat = chan_count * tiles_n * row_count
    yt_re = yt_re.reshape(flat, block)
    yt_im = yt_im.reshape(flat, block)
    s_re = (matmul_hi(yt_re, f_cos) + matmul_hi(yt_im, f_sin)) * row_scale
    s_im = (matmul_hi(yt_im, f_cos) - matmul_hi(yt_re, f_sin)) * row_scale
    s_re = s_re.reshape(chan_count, tiles_n, row_count, block)
    s_im = s_im.reshape(chan_count, tiles_n, row_count, block)
    z_re = jnp.einsum("ctrj,ctjm->ctrm", s_re, grid_tiles, precision=HI)
    z_im = jnp.einsum("ctrj,ctjm->ctrm", s_im, grid_tiles, precision=HI)
    place = jax.nn.one_hot(vis_block, vb_n, dtype=jnp.float32)
    r_re = jnp.einsum("ctv,ctrm->cvrm", place, z_re, precision=HI) - u_re
    r_im = jnp.einsum("ctv,ctrm->cvrm", place, z_im, precision=HI) - u_im
    sp_re = jnp.einsum("ctv,cvrm->ctrm", place, r_re, precision=HI)
    sp_im = jnp.einsum("ctv,cvrm->ctrm", place, r_im, precision=HI)
    c_re = jnp.einsum("ctrm,ctjm->ctrj", sp_re, grid_tiles, precision=HI)
    c_im = jnp.einsum("ctrm,ctjm->ctrj", sp_im, grid_tiles, precision=HI)
    c_re = c_re.reshape(flat, block)
    c_im = c_im.reshape(flat, block)
    d_re = (matmul_hi(c_re, f_cos) - matmul_hi(c_im, f_sin)) * row_scale
    d_im = (matmul_hi(c_re, f_sin) + matmul_hi(c_im, f_cos)) * row_scale
    d_re = d_re.reshape(chan_count, tiles_n, row_count, block)
    d_im = d_im.reshape(chan_count, tiles_n, row_count, block)
    dt_re = d_re * t_cos - d_im * t_sin
    dt_im = d_im * t_cos + d_re * t_sin
    return jnp.einsum("ctn,ctrm->ncrm", w_cos, dt_re, precision=HI) - jnp.einsum(
        "ctn,ctrm->ncrm", w_sin, dt_im, precision=HI
    )


def _on_device(sky_image, dual_field, sketch_matrix, grid_tiles, freq_block, vis_block, vis_data):
    chan_count, row_count, width = sky_image.shape
    block = grid_tiles.shape[2]
    blocks_n = width // block
    dual_b = lax.all_to_all(
        dual_field.reshape(blocks_n, chan_count, row_count, block), "chan", 0, 0, tiled=True
    )
    vis_all = exchange_gather(vis_data, "facet")
    sky_b = jnp.transpose(sky_image.reshape(chan_count, row_count, blocks_n, block), (2, 0, 1, 3))
    padded = padded_2(sky_b, (("facet", 2),), 1)
    grad_b = data_gradient(sky_b, grid_tiles, freq_block, vis_block, vis_all)
    smooth = 2.0 * sky_b - padded[:, :, :-2] - padded[:, :, 2:]
    new_b = sky_b - step_primal * (grad_b + smooth_weight * smooth + dual_b)
    new_image = jnp.transpose(new_b, (1, 2, 0, 3)).reshape(chan_count, row_count, width)
    rest = (1.0 - step_dual) * sky_b - 2.0 * step_dual * step_primal * (
        grad_b + smooth_weight * smooth
    )
    rest_pix = lax.all_to_all(rest, "chan", 0, 0, tiled=True).reshape(dual_field.shape)
    pixels = (1.0 - 2.0 * step_dual * step_primal) * dual_field + rest_pix
    chans = pixels.shape[0]
    flat_pix = pixels.reshape(chans, -1)
    sketch_rows = sketch_matrix.astype(jnp.float32).reshape(flat_pix.shape[1], -1)
    rank = sketch_rows.shape[1]
    part = jnp.concatenate(
        [matmul_hi(flat_pix, sketch_rows), jnp.dot(flat_pix, flat_pix.T, precision=HI)], axis=1
    )
    total = exchange_sum(part, "chan")
    sketch = total[:, :rank]
    outer = total[:, rank:]
    basis_mat = basis_transposed(matmul_hi(sketch.T, sketch), sketch.T).T
    gram_mat = matmul_hi(basis_mat.T, matmul_hi(outer, basis_mat))
    shrink = shrink_matrix(gram_mat)
    coords = matmul_hi(basis_mat.T, flat_pix)
    new_dual = flat_pix - matmul_hi(matmul_hi(basis_mat, shrink), coords)
    return (new_image, new_dual.reshape(pixels.shape))


def solution(mesh):
    placed = (
        P("chan", "facet", None),
        P(None, "facet", "chan"),
        P("facet", "chan", None),
        P("chan", None, None, None),
        P("chan", None),
        P("chan", None),
        P("chan", None, "facet", None, None),
    )
    return jax.shard_map(
        _on_device,
        mesh=mesh,
        in_specs=placed,
        out_specs=(P("chan", "facet", None), P(None, "facet", "chan")),
        check_vma=False,
    )
```

```python
import math

import jax
import jax.numpy as jnp
from jax import lax
from jax.sharding import PartitionSpec as P
from jax.experimental import pallas as pl
from jax.experimental.pallas import tpu as pltpu


SIGN_ITERS = 12
ROOT_ITERS = 14


step_primal = 0.4
smooth_weight = 0.25
step_dual = 0.5
shrink_ratio = 0.25

HI = lax.Precision.HIGHEST


def padded_2(block, sides, width):
    for axis, dim in sides:
        count = lax.axis_size(axis)
        forward = [(i, i + 1) for i in range(count - 1)]
        backward = [(target, source) for source, target in forward]
        low = lax.ppermute(
            lax.slice_in_dim(block, block.shape[dim] - width, None, axis=dim), axis, forward
        )
        high = lax.ppermute(lax.slice_in_dim(block, 0, width, axis=dim), axis, backward)
        block = jnp.concatenate([low, block, high], axis=dim)
    return block


def matmul_hi(first_mat, second_mat):
    return jnp.dot(first_mat, second_mat, precision=HI)


def shrink_matrix(gram_mat):
    order_n = gram_mat.shape[0]
    identity = jnp.eye(order_n, dtype=gram_mat.dtype)
    thresh_sq = shrink_ratio * jnp.trace(gram_mat) / order_n
    shifted = gram_mat - thresh_sq * identity
    signum = shifted / jnp.sqrt(jnp.sum(shifted * shifted))

    def iter_mm(first_mat, second_mat):
        return jnp.dot(first_mat, second_mat, precision=lax.Precision.HIGH)

    def sign_step(turn_no, current):
        return 1.5 * current - 0.5 * iter_mm(iter_mm(current, current), current)

    signum = lax.fori_loop(0, SIGN_ITERS, sign_step, signum, unroll=True)
    keeper = 0.5 * (identity + signum)
    floored = 0.5 * (gram_mat + thresh_sq * identity + matmul_hi(shifted, signum))
    scale_c = jnp.sqrt(jnp.sum(floored * floored))

    def root_step(turn_no, stacked):
        root_iter, inv_iter = stacked[:order_n], stacked[order_n:]
        step_mat = 0.5 * (3.0 * identity - iter_mm(inv_iter, root_iter))
        return iter_mm(stacked, step_mat)

    stacked = lax.fori_loop(
        0, ROOT_ITERS, root_step, jnp.concatenate([floored / scale_c, identity], axis=0), unroll=True
    )
    inv_iter = stacked[order_n:]
    inv_root = inv_iter / jnp.sqrt(scale_c)
    return matmul_hi(keeper, identity - jnp.sqrt(thresh_sq) * inv_root)


def _basis_kernel(gram_ref, side_ref, out_ref, work_ref, rhs_ref):
    order_n = gram_ref.shape[0]
    work_ref[...] = gram_ref[...]
    rhs_ref[...] = side_ref[...]
    lanes = lax.broadcasted_iota(jnp.int32, (1, order_n), 1)
    lanes_sq = lax.broadcasted_iota(jnp.int32, (order_n, order_n), 1)
    subs = lax.broadcasted_iota(jnp.int32, (order_n, 1), 0)

    def pick(vec, k):
        return jnp.sum(jnp.where(lanes == k, vec, 0.0), axis=1, keepdims=True)

    def step(t, carry):
        j = 2 * t
        row0 = work_ref[pl.ds(j, 1), :]
        row1 = work_ref[pl.ds(j + 1, 1), :]
        diag0 = jnp.sqrt(pick(row0, j))
        low10 = pick(row0, j + 1) / diag0
        diag1 = jnp.sqrt(pick(row1, j + 1) - low10 * low10)
        l_row0 = jnp.where(lanes >= j, row0, 0.0) / diag0
        l_row1 = jnp.where(lanes >= j + 1, row1 - l_row0 * low10, 0.0) / diag1
        work = work_ref[...]
        col0 = jnp.sum(jnp.where(lanes_sq == j, work, 0.0), axis=1, keepdims=True)
        col1 = jnp.sum(jnp.where(lanes_sq == j + 1, work, 0.0), axis=1, keepdims=True)
        l_col0 = jnp.where(subs >= j, col0, 0.0) / diag0
        l_col1 = jnp.where(subs >= j + 1, col1 - l_col0 * low10, 0.0) / diag1
        solved0 = rhs_ref[pl.ds(j, 1), :] / diag0
        solved1 = (rhs_ref[pl.ds(j + 1, 1), :] - low10 * solved0) / diag1
        out_ref[pl.ds(j, 1), :] = solved0
        out_ref[pl.ds(j + 1, 1), :] = solved1
        work_ref[...] = work - l_col0 * l_row0 - l_col1 * l_row1
        rhs_ref[...] = rhs_ref[...] - l_col0 * solved0 - l_col1 * solved1
        return carry

    lax.fori_loop(0, order_n // 2, step, 0)


def basis_transposed(gram_mat, side):
    order_n = gram_mat.shape[0]
    return pl.pallas_call(
        _basis_kernel,
        out_shape=jax.ShapeDtypeStruct(side.shape, jnp.float32),
        in_specs=[pl.BlockSpec(memory_space=pltpu.VMEM)] * 2,
        out_specs=pl.BlockSpec(memory_space=pltpu.VMEM),
        scratch_shapes=[
            pltpu.VMEM(gram_mat.shape, jnp.float32),
            pltpu.VMEM(side.shape, jnp.float32),
        ],
        cost_estimate=pl.CostEstimate(
            flops=4 * order_n * order_n * (order_n + side.shape[1]),
            transcendentals=order_n,
            bytes_accessed=4 * (order_n * order_n + 2 * side.size),
        ),
    )(gram_mat, side)


def phase_of(index, period):
    angle = (2.0 * math.pi / period) * (index % period).astype(jnp.float32)
    return jnp.cos(angle), jnp.sin(angle)


def exchange_sum(value, axis):
    count = lax.axis_size(axis)
    rows = value.shape[0]
    pieces = value.reshape((count, rows // count) + value.shape[1:])
    mine = jnp.sum(lax.all_to_all(pieces, axis, 0, 0, tiled=True), axis=0)
    spread = jnp.broadcast_to(mine[None], pieces.shape)
    return lax.all_to_all(spread, axis, 0, 0, tiled=True).reshape(value.shape)


def exchange_gather(value, axis):
    count = lax.axis_size(axis)
    spread = jnp.broadcast_to(value[None], (count,) + value.shape)
    return lax.all_to_all(spread, axis, 0, 0, tiled=True)


def data_gradient(sky_b, grid_tiles, freq_block, vis_block, vis_all):
    blocks_n, chan_count, row_count, block = sky_b.shape
    width = blocks_n * block
    n_facet = vis_all.shape[0]
    all_rows = n_facet * vis_all.shape[3]
    vb_n = vis_all.shape[4]
    row0 = lax.axis_index("facet") * row_count

    p_idx = lax.broadcasted_iota(jnp.int32, (row_count, n_facet, vis_all.shape[3]), 1) * vis_all.shape[
        3
    ] + lax.broadcasted_iota(jnp.int32, (row_count, n_facet, vis_all.shape[3]), 2)
    q_idx = lax.broadcasted_iota(jnp.int32, (row_count, n_facet, vis_all.shape[3]), 0) + row0
    cos_c, sin_c = phase_of(p_idx * q_idx, all_rows)
    col_scale = 1.0 / math.sqrt(all_rows)
    v_re = vis_all[:, :, 0]
    v_im = vis_all[:, :, 1]
    u_re = (
        jnp.einsum("qfp,fcpvm->cvqm", cos_c, v_re, precision=HI)
        - jnp.einsum("qfp,fcpvm->cvqm", sin_c, v_im, precision=HI)
    ) * col_scale
    u_im = (
        jnp.einsum("qfp,fcpvm->cvqm", sin_c, v_re, precision=HI)
        + jnp.einsum("qfp,fcpvm->cvqm", cos_c, v_im, precision=HI)
    ) * col_scale

    n2_idx = lax.broadcasted_iota(jnp.int32, freq_block.shape + (blocks_n,), 2)
    w_cos, w_sin = phase_of(freq_block[:, :, None] * n2_idx, blocks_n)
    n1_idx = lax.broadcasted_iota(jnp.int32, freq_block.shape + (block,), 2)
    t_cos, t_sin = phase_of(freq_block[:, :, None] * n1_idx, width)
    t_cos = t_cos[:, :, None, :]
    t_sin = t_sin[:, :, None, :]
    j_idx = lax.broadcasted_iota(jnp.int32, (block, block), 0)
    m_idx = lax.broadcasted_iota(jnp.int32, (block, block), 1)
    f_cos, f_sin = phase_of(j_idx * m_idx, block)
    row_scale = 1.0 / math.sqrt(width)

    y_re = jnp.einsum("ctn,ncrm->ctrm", w_cos, sky_b, precision=HI)
    y_im = -jnp.einsum("ctn,ncrm->ctrm", w_sin, sky_b, precision=HI)
    yt_re = y_re * t_cos + y_im * t_sin
    yt_im = y_im * t_cos - y_re * t_sin
    tiles_n = freq_block.shape[1]
    flat = chan_count * tiles_n * row_count
    yt_re = yt_re.reshape(flat, block)
    yt_im = yt_im.reshape(flat, block)
    s_re = (matmul_hi(yt_re, f_cos) + matmul_hi(yt_im, f_sin)) * row_scale
    s_im = (matmul_hi(yt_im, f_cos) - matmul_hi(yt_re, f_sin)) * row_scale
    s_re = s_re.reshape(chan_count, tiles_n, row_count, block)
    s_im = s_im.reshape(chan_count, tiles_n, row_count, block)
    z_re = jnp.einsum("ctrj,ctjm->ctrm", s_re, grid_tiles, precision=lax.Precision.HIGH)
    z_im = jnp.einsum("ctrj,ctjm->ctrm", s_im, grid_tiles, precision=lax.Precision.HIGH)
    place = jax.nn.one_hot(vis_block, vb_n, dtype=jnp.float32)
    r_re = jnp.einsum("ctv,ctrm->cvrm", place, z_re, precision=HI) - u_re
    r_im = jnp.einsum("ctv,ctrm->cvrm", place, z_im, precision=HI) - u_im
    sp_re = jnp.einsum("ctv,cvrm->ctrm", place, r_re, precision=HI)
    sp_im = jnp.einsum("ctv,cvrm->ctrm", place, r_im, precision=HI)
    c_re = jnp.einsum("ctrm,ctjm->ctrj", sp_re, grid_tiles, precision=lax.Precision.HIGH)
    c_im = jnp.einsum("ctrm,ctjm->ctrj", sp_im, grid_tiles, precision=lax.Precision.HIGH)
    c_re = c_re.reshape(flat, block)
    c_im = c_im.reshape(flat, block)
    d_re = (matmul_hi(c_re, f_cos) - matmul_hi(c_im, f_sin)) * row_scale
    d_im = (matmul_hi(c_re, f_sin) + matmul_hi(c_im, f_cos)) * row_scale
    d_re = d_re.reshape(chan_count, tiles_n, row_count, block)
    d_im = d_im.reshape(chan_count, tiles_n, row_count, block)
    dt_re = d_re * t_cos - d_im * t_sin
    dt_im = d_im * t_cos + d_re * t_sin
    return jnp.einsum("ctn,ctrm->ncrm", w_cos, dt_re, precision=HI) - jnp.einsum(
        "ctn,ctrm->ncrm", w_sin, dt_im, precision=HI
    )


def _on_device(sky_image, dual_field, sketch_matrix, grid_tiles, freq_block, vis_block, vis_data):
    chan_count, row_count, width = sky_image.shape
    block = grid_tiles.shape[2]
    blocks_n = width // block
    dual_b = lax.all_to_all(
        dual_field.reshape(blocks_n, chan_count, row_count, block), "chan", 0, 0, tiled=True
    )
    vis_all = exchange_gather(vis_data, "facet")
    sky_b = jnp.transpose(sky_image.reshape(chan_count, row_count, blocks_n, block), (2, 0, 1, 3))
    padded = padded_2(sky_b, (("facet", 2),), 1)
    grad_b = data_gradient(sky_b, grid_tiles, freq_block, vis_block, vis_all)
    smooth = 2.0 * sky_b - padded[:, :, :-2] - padded[:, :, 2:]
    new_b = sky_b - step_primal * (grad_b + smooth_weight * smooth + dual_b)
    new_image = jnp.transpose(new_b, (1, 2, 0, 3)).reshape(chan_count, row_count, width)
    rest = (1.0 - step_dual) * sky_b - 2.0 * step_dual * step_primal * (
        grad_b + smooth_weight * smooth
    )
    rest_pix = lax.all_to_all(rest, "chan", 0, 0, tiled=True).reshape(dual_field.shape)
    pixels = (1.0 - 2.0 * step_dual * step_primal) * dual_field + rest_pix
    chans = pixels.shape[0]
    flat_pix = pixels.reshape(chans, -1)
    sketch_rows = sketch_matrix.astype(jnp.float32).reshape(flat_pix.shape[1], -1)
    rank = sketch_rows.shape[1]
    part = jnp.concatenate(
        [matmul_hi(flat_pix, sketch_rows), jnp.dot(flat_pix, flat_pix.T, precision=HI)], axis=1
    )
    total = exchange_sum(part, "chan")
    sketch = total[:, :rank]
    outer = total[:, rank:]
    basis_mat = basis_transposed(matmul_hi(sketch.T, sketch), sketch.T).T
    gram_mat = matmul_hi(basis_mat.T, matmul_hi(outer, basis_mat))
    shrink = shrink_matrix(gram_mat)
    coords = matmul_hi(basis_mat.T, flat_pix)
    new_dual = flat_pix - matmul_hi(matmul_hi(basis_mat, shrink), coords)
    return (new_image, new_dual.reshape(pixels.shape))


def solution(mesh):
    placed = (
        P("chan", "facet", None),
        P(None, "facet", "chan"),
        P("facet", "chan", None),
        P("chan", None, None, None),
        P("chan", None),
        P("chan", None),
        P("chan", None, "facet", None, None),
    )
    return jax.shard_map(
        _on_device,
        mesh=mesh,
        in_specs=placed,
        out_specs=(P("chan", "facet", None), P(None, "facet", "chan")),
        check_vma=False,
    )
```

```python
import math

import jax
import jax.numpy as jnp
from jax import lax
from jax.sharding import PartitionSpec as P
from jax.experimental import pallas as pl
from jax.experimental.pallas import tpu as pltpu


SIGN_ITERS = 12
ROOT_ITERS = 14


step_primal = 0.4
smooth_weight = 0.25
step_dual = 0.5
shrink_ratio = 0.25

HI = lax.Precision.HIGHEST


def padded_2(block, sides, width):
    for axis, dim in sides:
        count = lax.axis_size(axis)
        forward = [(i, i + 1) for i in range(count - 1)]
        backward = [(target, source) for source, target in forward]
        low = lax.ppermute(
            lax.slice_in_dim(block, block.shape[dim] - width, None, axis=dim), axis, forward
        )
        high = lax.ppermute(lax.slice_in_dim(block, 0, width, axis=dim), axis, backward)
        block = jnp.concatenate([low, block, high], axis=dim)
    return block


def matmul_hi(first_mat, second_mat):
    return jnp.dot(first_mat, second_mat, precision=HI)


def matmul_lo(first_mat, second_mat):
    return jnp.dot(first_mat, second_mat, precision=lax.Precision.HIGH)


def shrink_matrix(gram_mat):
    order_n = gram_mat.shape[0]
    identity = jnp.eye(order_n, dtype=gram_mat.dtype)
    thresh_sq = shrink_ratio * jnp.trace(gram_mat) / order_n
    shifted = gram_mat - thresh_sq * identity
    signum = shifted / jnp.sqrt(jnp.sum(shifted * shifted))

    def iter_mm(first_mat, second_mat):
        return jnp.dot(first_mat, second_mat, precision=lax.Precision.HIGH)

    def sign_step(turn_no, current):
        return 1.5 * current - 0.5 * iter_mm(iter_mm(current, current), current)

    signum = lax.fori_loop(0, SIGN_ITERS, sign_step, signum, unroll=True)
    keeper = 0.5 * (identity + signum)
    floored = 0.5 * (gram_mat + thresh_sq * identity + matmul_hi(shifted, signum))
    scale_c = jnp.sqrt(jnp.sum(floored * floored))

    def root_step(turn_no, stacked):
        root_iter, inv_iter = stacked[:order_n], stacked[order_n:]
        step_mat = 0.5 * (3.0 * identity - iter_mm(inv_iter, root_iter))
        return iter_mm(stacked, step_mat)

    stacked = lax.fori_loop(
        0, ROOT_ITERS, root_step, jnp.concatenate([floored / scale_c, identity], axis=0), unroll=True
    )
    inv_iter = stacked[order_n:]
    inv_root = inv_iter / jnp.sqrt(scale_c)
    return matmul_hi(keeper, identity - jnp.sqrt(thresh_sq) * inv_root)


def _basis_kernel(gram_ref, side_ref, out_ref, work_ref, rhs_ref):
    order_n = gram_ref.shape[0]
    work_ref[...] = gram_ref[...]
    rhs_ref[...] = side_ref[...]
    lanes = lax.broadcasted_iota(jnp.int32, (1, order_n), 1)
    lanes_sq = lax.broadcasted_iota(jnp.int32, (order_n, order_n), 1)
    subs = lax.broadcasted_iota(jnp.int32, (order_n, 1), 0)

    def pick(vec, k):
        return jnp.sum(jnp.where(lanes == k, vec, 0.0), axis=1, keepdims=True)

    def step(t, carry):
        j = 2 * t
        row0 = work_ref[pl.ds(j, 1), :]
        row1 = work_ref[pl.ds(j + 1, 1), :]
        diag0 = jnp.sqrt(pick(row0, j))
        low10 = pick(row0, j + 1) / diag0
        diag1 = jnp.sqrt(pick(row1, j + 1) - low10 * low10)
        l_row0 = jnp.where(lanes >= j, row0, 0.0) / diag0
        l_row1 = jnp.where(lanes >= j + 1, row1 - l_row0 * low10, 0.0) / diag1
        work = work_ref[...]
        col0 = jnp.sum(jnp.where(lanes_sq == j, work, 0.0), axis=1, keepdims=True)
        col1 = jnp.sum(jnp.where(lanes_sq == j + 1, work, 0.0), axis=1, keepdims=True)
        l_col0 = jnp.where(subs >= j, col0, 0.0) / diag0
        l_col1 = jnp.where(subs >= j + 1, col1 - l_col0 * low10, 0.0) / diag1
        solved0 = rhs_ref[pl.ds(j, 1), :] / diag0
        solved1 = (rhs_ref[pl.ds(j + 1, 1), :] - low10 * solved0) / diag1
        out_ref[pl.ds(j, 1), :] = solved0
        out_ref[pl.ds(j + 1, 1), :] = solved1
        work_ref[...] = work - l_col0 * l_row0 - l_col1 * l_row1
        rhs_ref[...] = rhs_ref[...] - l_col0 * solved0 - l_col1 * solved1
        return carry

    lax.fori_loop(0, order_n // 2, step, 0)


def basis_transposed(gram_mat, side):
    order_n = gram_mat.shape[0]
    return pl.pallas_call(
        _basis_kernel,
        out_shape=jax.ShapeDtypeStruct(side.shape, jnp.float32),
        in_specs=[pl.BlockSpec(memory_space=pltpu.VMEM)] * 2,
        out_specs=pl.BlockSpec(memory_space=pltpu.VMEM),
        scratch_shapes=[
            pltpu.VMEM(gram_mat.shape, jnp.float32),
            pltpu.VMEM(side.shape, jnp.float32),
        ],
        cost_estimate=pl.CostEstimate(
            flops=4 * order_n * order_n * (order_n + side.shape[1]),
            transcendentals=order_n,
            bytes_accessed=4 * (order_n * order_n + 2 * side.size),
        ),
    )(gram_mat, side)


def phase_of(index, period):
    angle = (2.0 * math.pi / period) * (index % period).astype(jnp.float32)
    return jnp.cos(angle), jnp.sin(angle)


def exchange_sum(value, axis):
    count = lax.axis_size(axis)
    rows = value.shape[0]
    pieces = value.reshape((count, rows // count) + value.shape[1:])
    mine = jnp.sum(lax.all_to_all(pieces, axis, 0, 0, tiled=True), axis=0)
    spread = jnp.broadcast_to(mine[None], pieces.shape)
    return lax.all_to_all(spread, axis, 0, 0, tiled=True).reshape(value.shape)


def exchange_gather(value, axis):
    count = lax.axis_size(axis)
    spread = jnp.broadcast_to(value[None], (count,) + value.shape)
    return lax.all_to_all(spread, axis, 0, 0, tiled=True)


def data_gradient(sky_b, grid_tiles, freq_block, vis_block, vis_all):
    blocks_n, chan_count, row_count, block = sky_b.shape
    width = blocks_n * block
    n_facet = vis_all.shape[0]
    all_rows = n_facet * vis_all.shape[3]
    vb_n = vis_all.shape[4]
    row0 = lax.axis_index("facet") * row_count

    p_idx = lax.broadcasted_iota(jnp.int32, (row_count, n_facet, vis_all.shape[3]), 1) * vis_all.shape[
        3
    ] + lax.broadcasted_iota(jnp.int32, (row_count, n_facet, vis_all.shape[3]), 2)
    q_idx = lax.broadcasted_iota(jnp.int32, (row_count, n_facet, vis_all.shape[3]), 0) + row0
    cos_c, sin_c = phase_of(p_idx * q_idx, all_rows)
    col_scale = 1.0 / math.sqrt(all_rows)
    v_re = vis_all[:, :, 0]
    v_im = vis_all[:, :, 1]
    u_re = (
        jnp.einsum("qfp,fcpvm->cvqm", cos_c, v_re, precision=HI)
        - jnp.einsum("qfp,fcpvm->cvqm", sin_c, v_im, precision=HI)
    ) * col_scale
    u_im = (
        jnp.einsum("qfp,fcpvm->cvqm", sin_c, v_re, precision=HI)
        + jnp.einsum("qfp,fcpvm->cvqm", cos_c, v_im, precision=HI)
    ) * col_scale

    n2_idx = lax.broadcasted_iota(jnp.int32, freq_block.shape + (blocks_n,), 2)
    w_cos, w_sin = phase_of(freq_block[:, :, None] * n2_idx, blocks_n)
    n1_idx = lax.broadcasted_iota(jnp.int32, freq_block.shape + (block,), 2)
    t_cos, t_sin = phase_of(freq_block[:, :, None] * n1_idx, width)
    t_cos = t_cos[:, :, None, :]
    t_sin = t_sin[:, :, None, :]
    j_idx = lax.broadcasted_iota(jnp.int32, (block, block), 0)
    m_idx = lax.broadcasted_iota(jnp.int32, (block, block), 1)
    f_cos, f_sin = phase_of(j_idx * m_idx, block)
    row_scale = 1.0 / math.sqrt(width)

    y_re = jnp.einsum("ctn,ncrm->ctrm", w_cos, sky_b, precision=lax.Precision.HIGH)
    y_im = -jnp.einsum("ctn,ncrm->ctrm", w_sin, sky_b, precision=lax.Precision.HIGH)
    yt_re = y_re * t_cos + y_im * t_sin
    yt_im = y_im * t_cos - y_re * t_sin
    tiles_n = freq_block.shape[1]
    flat = chan_count * tiles_n * row_count
    yt_re = yt_re.reshape(flat, block)
    yt_im = yt_im.reshape(flat, block)
    s_re = (matmul_lo(yt_re, f_cos) + matmul_lo(yt_im, f_sin)) * row_scale
    s_im = (matmul_lo(yt_im, f_cos) - matmul_lo(yt_re, f_sin)) * row_scale
    s_re = s_re.reshape(chan_count, tiles_n, row_count, block)
    s_im = s_im.reshape(chan_count, tiles_n, row_count, block)
    z_re = jnp.einsum("ctrj,ctjm->ctrm", s_re, grid_tiles, precision=lax.Precision.HIGH)
    z_im = jnp.einsum("ctrj,ctjm->ctrm", s_im, grid_tiles, precision=lax.Precision.HIGH)
    place = jax.nn.one_hot(vis_block, vb_n, dtype=jnp.float32)
    r_re = jnp.einsum("ctv,ctrm->cvrm", place, z_re, precision=lax.Precision.HIGH) - u_re
    r_im = jnp.einsum("ctv,ctrm->cvrm", place, z_im, precision=lax.Precision.HIGH) - u_im
    sp_re = jnp.einsum("ctv,cvrm->ctrm", place, r_re, precision=lax.Precision.HIGH)
    sp_im = jnp.einsum("ctv,cvrm->ctrm", place, r_im, precision=lax.Precision.HIGH)
    c_re = jnp.einsum("ctrm,ctjm->ctrj", sp_re, grid_tiles, precision=lax.Precision.HIGH)
    c_im = jnp.einsum("ctrm,ctjm->ctrj", sp_im, grid_tiles, precision=lax.Precision.HIGH)
    c_re = c_re.reshape(flat, block)
    c_im = c_im.reshape(flat, block)
    d_re = (matmul_lo(c_re, f_cos) - matmul_lo(c_im, f_sin)) * row_scale
    d_im = (matmul_lo(c_re, f_sin) + matmul_lo(c_im, f_cos)) * row_scale
    d_re = d_re.reshape(chan_count, tiles_n, row_count, block)
    d_im = d_im.reshape(chan_count, tiles_n, row_count, block)
    dt_re = d_re * t_cos - d_im * t_sin
    dt_im = d_im * t_cos + d_re * t_sin
    return jnp.einsum("ctn,ctrm->ncrm", w_cos, dt_re, precision=lax.Precision.HIGH) - jnp.einsum(
        "ctn,ctrm->ncrm", w_sin, dt_im, precision=HI
    )


def _on_device(sky_image, dual_field, sketch_matrix, grid_tiles, freq_block, vis_block, vis_data):
    chan_count, row_count, width = sky_image.shape
    block = grid_tiles.shape[2]
    blocks_n = width // block
    dual_b = lax.all_to_all(
        dual_field.reshape(blocks_n, chan_count, row_count, block), "chan", 0, 0, tiled=True
    )
    vis_all = exchange_gather(vis_data, "facet")
    sky_b = jnp.transpose(sky_image.reshape(chan_count, row_count, blocks_n, block), (2, 0, 1, 3))
    padded = padded_2(sky_b, (("facet", 2),), 1)
    grad_b = data_gradient(sky_b, grid_tiles, freq_block, vis_block, vis_all)
    smooth = 2.0 * sky_b - padded[:, :, :-2] - padded[:, :, 2:]
    new_b = sky_b - step_primal * (grad_b + smooth_weight * smooth + dual_b)
    new_image = jnp.transpose(new_b, (1, 2, 0, 3)).reshape(chan_count, row_count, width)
    rest = (1.0 - step_dual) * sky_b - 2.0 * step_dual * step_primal * (
        grad_b + smooth_weight * smooth
    )
    rest_pix = lax.all_to_all(rest, "chan", 0, 0, tiled=True).reshape(dual_field.shape)
    pixels = (1.0 - 2.0 * step_dual * step_primal) * dual_field + rest_pix
    chans = pixels.shape[0]
    flat_pix = pixels.reshape(chans, -1)
    sketch_rows = sketch_matrix.astype(jnp.float32).reshape(flat_pix.shape[1], -1)
    rank = sketch_rows.shape[1]
    part = jnp.concatenate(
        [matmul_hi(flat_pix, sketch_rows), jnp.dot(flat_pix, flat_pix.T, precision=HI)], axis=1
    )
    total = exchange_sum(part, "chan")
    sketch = total[:, :rank]
    outer = total[:, rank:]
    basis_mat = basis_transposed(matmul_hi(sketch.T, sketch), sketch.T).T
    gram_mat = matmul_hi(basis_mat.T, matmul_hi(outer, basis_mat))
    shrink = shrink_matrix(gram_mat)
    coords = matmul_hi(basis_mat.T, flat_pix)
    new_dual = flat_pix - matmul_hi(matmul_hi(basis_mat, shrink), coords)
    return (new_image, new_dual.reshape(pixels.shape))


def solution(mesh):
    placed = (
        P("chan", "facet", None),
        P(None, "facet", "chan"),
        P("facet", "chan", None),
        P("chan", None, None, None),
        P("chan", None),
        P("chan", None),
        P("chan", None, "facet", None, None),
    )
    return jax.shard_map(
        _on_device,
        mesh=mesh,
        in_specs=placed,
        out_specs=(P("chan", "facet", None), P(None, "facet", "chan")),
        check_vma=False,
    )
```
